32 devices in a mesh: dp: 2 (over x), ctx: 4 (over z), tensor: 4 (over y, core).
Axes of the slice: x: 2, y: 2, z: 4, core: 2. Of those that a mesh axis runs over, the one named last changes fastest.
Arguments:
- queries: bfloat16 [2, 1024, 2048], P('dp', 'ctx', 'tensor'), may hold values from -32 to 32
- keyvals: bfloat16 [2, 1024, 2, 512], P('dp', 'ctx', None, 'tensor'), may hold values from -32 to 32
- documents: int32 [2, 1024], P('dp', 'ctx'), may hold values from 0 to 18, as said below
- output_weight: bfloat16 [2048, 4096], P(('dp', 'ctx'), 'tensor'), may hold values from -0.125 to 0.125
Outputs:
- projected: bfloat16 [2, 1024, 4096], P('dp', 'ctx', 'tensor')
The draws below stay inside these ranges and needn't reach their ends.
Inputs may be any that keep to these rules, and one draw needn't show every extreme that they name: In each window the document numbers start at 0, never fall and rise by at most one from a position to the next; a window holds exactly 19 documents; no document holds more than 512 positions, and one holds exactly 512.
All inputs are finite; a program needn't handle non-finite values.
Results may differ from the reference program's by a relative error of at most 0.0051.
Values may be sent and summed in bfloat16 or wider, within the bound.
No kernel may reach another device: no remote copies, remote signals or barrier semaphores. Data moves between devices by JAX's collectives and lax.ppermute only.
A program may use at most 64 MiB of HBM per device.

```python
import math
import jax
import jax.numpy as jnp
from jax import lax

D = 4096
HEAD_DIM = 128
QUERY_HEADS = 16
KEY_VALUE_HEADS = 4
WINDOW_LENGTH = 1024
WINDOW_COUNT = 2
MOST = 512


def doc_numbers(key):
    cut_count = WINDOW_LENGTH // 64

    def one_window(window_key):
        begin_key, cut_key = jax.random.split(window_key)
        begin = jax.random.randint(begin_key, (), 1, WINDOW_LENGTH - MOST)
        places = jnp.arange(WINDOW_LENGTH, dtype=jnp.int32)
        outside = (places < begin) | (places >= begin + MOST)
        candidate = outside & (places != 0) & (places != begin + MOST)
        scores = jax.random.randint(cut_key, (WINDOW_LENGTH,), 0, 1 << 15) * WINDOW_LENGTH + places
        scores = jnp.where(candidate, scores, -1)
        selected_rows = lax.top_k(scores, cut_count)[1]
        cuts = jnp.zeros((WINDOW_LENGTH,), jnp.int32).at[selected_rows].set(1) > 0
        starts = (places == 0) | (places == begin) | (places == begin + MOST) | cuts
        return (jnp.cumsum(starts.astype(jnp.int32)) - 1).astype(jnp.int32)
    return jax.vmap(one_window)(jax.random.split(key, WINDOW_COUNT))


def key_values(key):
    array_shape = (WINDOW_COUNT, WINDOW_LENGTH, KEY_VALUE_HEADS * HEAD_DIM)
    key_rows = 2.5 * jnp.clip(jax.random.normal(jax.random.fold_in(key, 31), array_shape, jnp.float32), -6.0, 6.0)
    values = jnp.clip(jax.random.normal(jax.random.fold_in(key, 33), array_shape, jnp.float32), -6.0, 6.0)
    return (key_rows, values)


def draw_keyvals(key, part):
    key_rows, values = key_values(key)
    return jnp.stack([key_rows, values], axis=2).astype(jnp.bfloat16)


def draw_queries(key, part):
    array_shape = (WINDOW_COUNT, WINDOW_LENGTH, QUERY_HEADS * HEAD_DIM)
    base = jnp.clip(jax.random.normal(jax.random.fold_in(key, 21), array_shape, jnp.float32), -6.0, 6.0)
    return base.astype(jnp.bfloat16)


def draw_documents(key, part):
    return doc_numbers(jax.random.fold_in(key, 11))


def shard_levels(key, shape, cuts, low, high):
    def one(position, shards_of):
        heights = jax.random.uniform(jax.random.fold_in(jax.random.fold_in(key, 6), position), (shards_of,), jnp.float32, low / len(cuts), high / len(cuts))
        return jnp.repeat(jnp.exp(heights), shape[position] // shards_of).reshape((-1,) + (1,) * (len(shape) - position - 1))

    gain = one(*cuts[0])
    for cut in cuts[1:]:
        gain = gain * one(*cut)
    return gain


def gaussian(key, extent, spread, limit, pieces=(), held_as=jnp.bfloat16):
    values = spread * jax.random.normal(key, extent, jnp.float32)
    if pieces:
        values = values * shard_levels(key, extent, pieces, -0.22, 0.18)
    return jnp.clip(values, -limit, limit).astype(held_as)


def setup_inputs(seed: int = 0) -> dict:
    arg_keys = jax.random.split(jax.random.key(seed), 5)
    queries = draw_queries(jax.random.fold_in(arg_keys[4], 71), 0)
    keyvals = draw_keyvals(jax.random.fold_in(arg_keys[4], 71), 0)
    documents = draw_documents(jax.random.fold_in(arg_keys[4], 71), 0)
    output_weight = gaussian(arg_keys[3], (QUERY_HEADS * HEAD_DIM, D), (QUERY_HEADS * HEAD_DIM) ** -0.5, 0.125, ((0, 8), (1, 4)))
    return dict(queries=queries, keyvals=keyvals, documents=documents, output_weight=output_weight)


FLOOR_SCORE = -1e+30

def one_window(queries_w, key_value_weight, labels_w):
    query_group_size = QUERY_HEADS // KEY_VALUE_HEADS
    block_row_count = min(128, WINDOW_LENGTH // 2)
    span = MOST + block_row_count
    gathered_keys = key_value_weight[:, 0].astype(jnp.float32).reshape(WINDOW_LENGTH, KEY_VALUE_HEADS, HEAD_DIM)
    gathered_values = key_value_weight[:, 1].astype(jnp.float32).reshape(WINDOW_LENGTH, KEY_VALUE_HEADS, HEAD_DIM)

    def one_block(block_index):
        first_row = (block_index * block_row_count).astype(jnp.int32)
        first_key = jnp.clip(first_row + block_row_count - span, 0, WINDOW_LENGTH - span).astype(jnp.int32)
        query_slice = lax.dynamic_slice_in_dim(queries_w, first_row, block_row_count, 0)
        query_slice = query_slice.astype(jnp.float32).reshape(block_row_count, KEY_VALUE_HEADS, query_group_size, HEAD_DIM)
        key_part = lax.dynamic_slice_in_dim(gathered_keys, first_key, span, 0)
        value_part = lax.dynamic_slice_in_dim(gathered_values, first_key, span, 0)
        query_labels = lax.dynamic_slice_in_dim(labels_w, first_row, block_row_count, 0)
        key_labels = lax.dynamic_slice_in_dim(labels_w, first_key, span, 0)
        query_place = first_row + jnp.arange(block_row_count, dtype=jnp.int32)
        key_place = first_key + jnp.arange(span, dtype=jnp.int32)
        allowed = (query_labels[:, None] == key_labels[None, :]) & (key_place[None, :] <= query_place[:, None])
        scores = jnp.einsum('qhgd,khd->hgqk', query_slice, key_part) * (1.0 / math.sqrt(HEAD_DIM))
        scores = jnp.where(allowed, scores, FLOOR_SCORE)
        peak = lax.optimization_barrier(jnp.max(scores, axis=-1, keepdims=True))
        exp_terms = jnp.where(allowed, jnp.exp(scores - peak), 0.0)
        totals = lax.optimization_barrier(jnp.sum(exp_terms, axis=-1))
        weights = lax.optimization_barrier(exp_terms.astype(jnp.bfloat16))
        summed = jnp.einsum('hgqk,khd->qhgd', weights.astype(jnp.float32), value_part)
        head_values = summed / jnp.transpose(totals, (2, 0, 1))[..., None]
        return head_values.reshape(block_row_count, QUERY_HEADS * HEAD_DIM).astype(jnp.bfloat16)
    blocks = lax.map(one_block, jnp.arange(WINDOW_LENGTH // block_row_count, dtype=jnp.int32))
    return blocks.reshape(WINDOW_LENGTH, QUERY_HEADS * HEAD_DIM)

def reference(queries, keyvals, documents, output_weight):
    head_values = lax.map(lambda parts: one_window(parts[0], parts[1], parts[2]), (queries, keyvals, documents))
    flat = head_values.reshape(WINDOW_COUNT * WINDOW_LENGTH, QUERY_HEADS * HEAD_DIM)
    result = jnp.dot(flat, output_weight, preferred_element_type=jnp.float32)
    return result.astype(jnp.bfloat16).reshape(WINDOW_COUNT, WINDOW_LENGTH, D)
```

```python
import math

import jax
import jax.numpy as jnp
from jax import lax
from jax.sharding import PartitionSpec as P

HEAD_DIM = 128


FLOOR_SCORE = -1e30


def shifted(block, axis, distance):
    devices = range(lax.axis_size(axis))
    route = [(i - distance, i) for i in devices if i - distance in devices]
    return lax.ppermute(block, axis, route)


def rotated(block, axis, distance):
    count = lax.axis_size(axis)
    route = [(i, (i + distance) % count) for i in range(count)]
    return lax.ppermute(block, axis, route)


def attention(queries, keyvals, documents):
    length = queries.shape[1]
    pair_width = keyvals.shape[3]
    pair_heads = pair_width // HEAD_DIM
    query_group_size = queries.shape[2] // pair_width
    cycle_size = lax.axis_size("ctx")
    position = lax.axis_index("ctx")
    offsets = jnp.arange(length, dtype=jnp.int32)
    reach_hops = min(cycle_size - 1, (cycle_size * length // 2 - 1 + length - 1) // length)

    pair_blocks = [keyvals[0]]
    label_blocks = [documents[0]]
    place_blocks = [position * length + offsets]
    for hop in range(1, reach_hops + 1):
        pair_block, label_block = shifted((keyvals[0], documents[0]), "ctx", hop)
        pair_blocks.append(pair_block)
        label_blocks.append(label_block)
        place_blocks.append((position - hop) * length + offsets)
    pairs = jnp.concatenate(pair_blocks, axis=0)
    key_labels = jnp.concatenate(label_blocks, axis=0)
    key_place = jnp.concatenate(place_blocks, axis=0)
    key_count = pairs.shape[0]

    query_place = position * length + offsets
    query_labels = documents[0]
    query_block = queries[0].reshape(length, pair_heads, query_group_size, HEAD_DIM)
    key_block = pairs[:, 0].reshape(key_count, pair_heads, HEAD_DIM)
    value_block = pairs[:, 1].reshape(key_count, pair_heads, HEAD_DIM)

    scores = jnp.einsum(
        "qhgd,khd->hgqk", query_block, key_block, preferred_element_type=jnp.float32
    )
    scores = scores * (1.0 / math.sqrt(HEAD_DIM))
    allowed = (
        (query_labels[:, None] == key_labels[None, :])
        & (key_place[None, :] <= query_place[:, None])
        & (key_place[None, :] >= 0)
    )
    scores = jnp.where(allowed, scores, FLOOR_SCORE)
    peak = jnp.max(scores, axis=-1, keepdims=True)
    expo = jnp.where(allowed, jnp.exp(scores - peak), 0.0)
    total = jnp.sum(expo, axis=-1)
    summed = jnp.einsum(
        "hgqk,khd->qhgd",
        expo.astype(jnp.bfloat16),
        value_block,
        preferred_element_type=jnp.float32,
    )
    head_values = summed / jnp.transpose(total, (2, 0, 1))[..., None]
    return head_values.reshape(length, pair_heads * query_group_size * HEAD_DIM).astype(
        jnp.bfloat16
    )


def shards(queries, keyvals, documents, output_weight):
    all_rows = lax.all_gather(output_weight, ("dp", "ctx"), axis=0, tiled=True)
    head_values = attention(queries, keyvals, documents)
    width = head_values.shape[1]
    group = lax.axis_size("tensor")
    me = lax.axis_index("tensor")
    result = None
    for distance in range(group):
        held = head_values if distance == 0 else rotated(head_values, "tensor", distance)
        owner = (me - distance) % group
        rows = lax.dynamic_slice_in_dim(all_rows, owner * width, width, 0)
        part = jnp.dot(held, rows, preferred_element_type=jnp.float32)
        result = part if result is None else result + part
    return result.astype(jnp.bfloat16)[None]


def solution(mesh):
    placed = (
        P("dp", "ctx", "tensor"),
        P("dp", "ctx", None, "tensor"),
        P("dp", "ctx"),
        P(("dp", "ctx"), "tensor"),
    )
    return jax.shard_map(
        shards, mesh=mesh, in_specs=placed, out_specs=P("dp", "ctx", "tensor"), check_vma=False
    )
```

```python
import math

import jax
import jax.numpy as jnp
from jax import lax
from jax.sharding import PartitionSpec as P

HEAD_DIM = 128


FLOOR_SCORE = -1e30


def shifted(block, axis, distance):
    devices = range(lax.axis_size(axis))
    route = [(i - distance, i) for i in devices if i - distance in devices]
    return lax.ppermute(block, axis, route)


def rotated(block, axis, distance):
    count = lax.axis_size(axis)
    route = [(i, (i + distance) % count) for i in range(count)]
    return lax.ppermute(block, axis, route)


def attention(queries, keyvals, documents):
    length = queries.shape[1]
    pair_width = keyvals.shape[3]
    pair_heads = pair_width // HEAD_DIM
    query_group_size = queries.shape[2] // pair_width
    cycle_size = lax.axis_size("ctx")
    position = lax.axis_index("ctx")
    offsets = jnp.arange(length, dtype=jnp.int32)
    reach_hops = min(cycle_size - 1, (cycle_size * length // 2 - 1 + length - 1) // length)

    pair_blocks = [keyvals[0]]
    label_blocks = [documents[0]]
    place_blocks = [position * length + offsets]
    for hop in range(1, reach_hops + 1):
        pair_block, label_block = shifted((keyvals[0], documents[0]), "ctx", hop)
        pair_blocks.append(pair_block)
        label_blocks.append(label_block)
        place_blocks.append((position - hop) * length + offsets)
    pairs = jnp.concatenate(pair_blocks, axis=0)
    key_labels = jnp.concatenate(label_blocks, axis=0)
    key_place = jnp.concatenate(place_blocks, axis=0)
    key_count = pairs.shape[0]

    query_place = position * length + offsets
    query_labels = documents[0]
    query_block = queries[0].reshape(length, pair_heads, query_group_size, HEAD_DIM)
    key_block = pairs[:, 0].reshape(key_count, pair_heads, HEAD_DIM)
    value_block = pairs[:, 1].reshape(key_count, pair_heads, HEAD_DIM)

    scores = jnp.einsum(
        "qhgd,khd->hgqk", query_block, key_block, preferred_element_type=jnp.float32
    )
    scores = scores * (1.0 / math.sqrt(HEAD_DIM))
    allowed = (
        (query_labels[:, None] == key_labels[None, :])
        & (key_place[None, :] <= query_place[:, None])
        & (key_place[None, :] >= 0)
    )
    scores = jnp.where(allowed, scores, FLOOR_SCORE)
    peak = jnp.max(scores, axis=-1, keepdims=True)
    expo = jnp.where(allowed, jnp.exp(scores - peak), 0.0)
    total = jnp.sum(expo, axis=-1)
    summed = jnp.einsum(
        "hgqk,khd->qhgd",
        expo.astype(jnp.bfloat16),
        value_block,
        preferred_element_type=jnp.float32,
    )
    head_values = summed / jnp.transpose(total, (2, 0, 1))[..., None]
    return head_values.reshape(length, pair_heads * query_group_size * HEAD_DIM).astype(
        jnp.bfloat16
    )


def line_blocks(block, axis):
    count = lax.axis_size(axis)
    upward = [(block, 0)]
    downward = []
    rising, falling = block, block
    for step in range(1, count):
        rising = lax.ppermute(rising, axis, [(i, i + 1) for i in range(step - 1, count - 1)])
        falling = lax.ppermute(falling, axis, [(i, i - 1) for i in range(1, count - step + 1)])
        upward.append((rising, -step))
        downward.append((falling, step))
    return upward + downward


def crossed(block, count, holders):
    route = [(side * count + c, (1 - side) * count + c) for side in range(2) for c in holders]
    return lax.ppermute(block, ("dp", "ctx"), route)


def forwarded_rows(output_weight):
    count = lax.axis_size("ctx")
    side = lax.axis_index("dp")
    here = lax.axis_index("ctx")
    pieces = []
    for block, offset in line_blocks(output_weight, "ctx"):
        if offset > 0:
            holders = range(0, count - offset)
        else:
            holders = range(-offset, count)
        pieces.append((block, side * count + here + offset))
        pieces.append((crossed(block, count, holders), (1 - side) * count + here + offset))
    return pieces


def shards(queries, keyvals, documents, output_weight):
    block_rows = output_weight.shape[0]
    width = queries.shape[2]
    pipelined = lax.axis_size("dp") == 2 and width % block_rows == 0
    if pipelined:
        pieces = forwarded_rows(output_weight)
    else:
        all_rows = lax.all_gather(output_weight, ("dp", "ctx"), axis=0, tiled=True)
    head_values = attention(queries, keyvals, documents)
    group = lax.axis_size("tensor")
    me = lax.axis_index("tensor")
    held = [head_values] + [rotated(head_values, "tensor", d) for d in range(1, group)]
    result = None
    if pipelined:
        heads_rel = jnp.concatenate(held, axis=1)
        last_block = lax.axis_size("dp") * lax.axis_size("ctx") - 1
        for block, row_block in pieces:
            row_block = jnp.clip(row_block, 0, last_block)
            first_row = row_block * block_rows
            owner = first_row // width
            column = ((me - owner) % group) * width + first_row % width
            columns = lax.dynamic_slice_in_dim(heads_rel, column, block_rows, 1)
            part = jnp.dot(columns, block, preferred_element_type=jnp.float32)
            result = part if result is None else result + part
    else:
        for distance in range(group):
            owner = (me - distance) % group
            rows = lax.dynamic_slice_in_dim(all_rows, owner * width, width, 0)
            part = jnp.dot(held[distance], rows, preferred_element_type=jnp.float32)
            result = part if result is None else result + part
    return result.astype(jnp.bfloat16)[None]


def solution(mesh):
    placed = (
        P("dp", "ctx", "tensor"),
        P("dp", "ctx", None, "tensor"),
        P("dp", "ctx"),
        P(("dp", "ctx"), "tensor"),
    )
    return jax.shard_map(
        shards, mesh=mesh, in_specs=placed, out_specs=P("dp", "ctx", "tensor"), check_vma=False
    )
```

```python
import math

import jax
import jax.numpy as jnp
from jax import lax
from jax.sharding import PartitionSpec as P

HEAD_DIM = 128


FLOOR_SCORE = -1e30


def shifted(block, axis, distance):
    devices = range(lax.axis_size(axis))
    route = [(i - distance, i) for i in devices if i - distance in devices]
    return lax.ppermute(block, axis, route)


def rotated(block, axis, distance):
    count = lax.axis_size(axis)
    route = [(i, (i + distance) % count) for i in range(count)]
    return lax.ppermute(block, axis, route)


def attention(queries, keyvals, documents):
    length = queries.shape[1]
    pair_width = keyvals.shape[3]
    pair_heads = pair_width // HEAD_DIM
    query_group_size = queries.shape[2] // pair_width
    cycle_size = lax.axis_size("ctx")
    position = lax.axis_index("ctx")
    offsets = jnp.arange(length, dtype=jnp.int32)
    reach_hops = min(cycle_size - 1, (cycle_size * length // 2 - 1 + length - 1) // length)

    pair_blocks = [keyvals[0]]
    label_blocks = [documents[0]]
    place_blocks = [position * length + offsets]
    for hop in range(1, reach_hops + 1):
        pair_block, label_block = shifted((keyvals[0], documents[0]), "ctx", hop)
        pair_blocks.append(pair_block)
        label_blocks.append(label_block)
        place_blocks.append((position - hop) * length + offsets)
    pairs = jnp.concatenate(pair_blocks, axis=0)
    key_labels = jnp.concatenate(label_blocks, axis=0)
    key_place = jnp.concatenate(place_blocks, axis=0)
    key_count = pairs.shape[0]

    query_place = position * length + offsets
    query_labels = documents[0]
    query_block = queries[0].reshape(length, pair_heads, query_group_size, HEAD_DIM)
    key_block = pairs[:, 0].reshape(key_count, pair_heads, HEAD_DIM)
    value_block = pairs[:, 1].reshape(key_count, pair_heads, HEAD_DIM)

    scores = jnp.einsum(
        "qhgd,khd->hgqk", query_block, key_block, preferred_element_type=jnp.float32
    )
    scores = scores * (1.0 / math.sqrt(HEAD_DIM))
    allowed = (
        (query_labels[:, None] == key_labels[None, :])
        & (key_place[None, :] <= query_place[:, None])
        & (key_place[None, :] >= 0)
    )
    scores = jnp.where(allowed, scores, FLOOR_SCORE)
    peak = jnp.max(scores, axis=-1, keepdims=True)
    expo = jnp.where(allowed, jnp.exp(scores - peak), 0.0)
    total = jnp.sum(expo, axis=-1)
    summed = jnp.einsum(
        "hgqk,khd->qhgd",
        expo.astype(jnp.bfloat16),
        value_block,
        preferred_element_type=jnp.float32,
    )
    head_values = summed / jnp.transpose(total, (2, 0, 1))[..., None]
    return head_values.reshape(length, pair_heads * query_group_size * HEAD_DIM).astype(
        jnp.bfloat16
    )


def swapped(block, axis):
    return lax.ppermute(block, axis, [(0, 1), (1, 0)])


def split_projection(head_values, output_weight):
    block_rows = output_weight.shape[0]
    width = head_values.shape[1]
    group = lax.axis_size("tensor")
    me = lax.axis_index("tensor")
    side = lax.axis_index("dp")
    side_rows = lax.all_gather(output_weight, "ctx", axis=0, tiled=True)
    side_width = side_rows.shape[0]
    foreign = swapped(head_values, "dp")
    both = jnp.concatenate([head_values, foreign], axis=1)
    held = [both] + [rotated(both, "tensor", d) for d in range(1, group)]
    mixed = jnp.concatenate(held, axis=1)
    local = None
    partner = None
    for j in range(side_width // width):
        owner = side * (side_width // width) + j
        column = ((me - owner) % group) * (2 * width)
        own_part = lax.dynamic_slice_in_dim(mixed, column, width, 1)
        their_part = lax.dynamic_slice_in_dim(mixed, column + width, width, 1)
        rows = side_rows[j * width:(j + 1) * width]
        mine = jnp.dot(own_part, rows, preferred_element_type=jnp.float32)
        theirs = jnp.dot(their_part, rows, preferred_element_type=jnp.float32)
        local = mine if local is None else local + mine
        partner = theirs if partner is None else partner + theirs
    returned = swapped(partner.astype(jnp.bfloat16), "dp")
    return local + returned.astype(jnp.float32)


def shards(queries, keyvals, documents, output_weight):
    block_rows = output_weight.shape[0]
    width = queries.shape[2]
    side_width = block_rows * lax.axis_size("ctx")
    if lax.axis_size("dp") == 2 and side_width % width == 0:
        head_values = attention(queries, keyvals, documents)
        result = split_projection(head_values, output_weight)
        return result.astype(jnp.bfloat16)[None]
    all_rows = lax.all_gather(output_weight, ("dp", "ctx"), axis=0, tiled=True)
    head_values = attention(queries, keyvals, documents)
    group = lax.axis_size("tensor")
    me = lax.axis_index("tensor")
    result = None
    for distance in range(group):
        held = head_values if distance == 0 else rotated(head_values, "tensor", distance)
        owner = (me - distance) % group
        rows = lax.dynamic_slice_in_dim(all_rows, owner * width, width, 0)
        part = jnp.dot(held, rows, preferred_element_type=jnp.float32)
        result = part if result is None else result + part
    return result.astype(jnp.bfloat16)[None]


def solution(mesh):
    placed = (
        P("dp", "ctx", "tensor"),
        P("dp", "ctx", None, "tensor"),
        P("dp", "ctx"),
        P(("dp", "ctx"), "tensor"),
    )
    return jax.shard_map(
        shards, mesh=mesh, in_specs=placed, out_specs=P("dp", "ctx", "tensor"), check_vma=False
    )
```

```python
import math

import jax
import jax.numpy as jnp
from jax import lax
from jax.sharding import PartitionSpec as P

HEAD_DIM = 128


FLOOR_SCORE = -1e30


def shifted(block, axis, distance):
    devices = range(lax.axis_size(axis))
    route = [(i - distance, i) for i in devices if i - distance in devices]
    return lax.ppermute(block, axis, route)


def rotated(block, axis, distance):
    count = lax.axis_size(axis)
    route = [(i, (i + distance) % count) for i in range(count)]
    return lax.ppermute(block, axis, route)


def attention(queries, keyvals, documents):
    length = queries.shape[1]
    pair_width = keyvals.shape[3]
    pair_heads = pair_width // HEAD_DIM
    query_group_size = queries.shape[2] // pair_width
    cycle_size = lax.axis_size("ctx")
    position = lax.axis_index("ctx")
    offsets = jnp.arange(length, dtype=jnp.int32)
    reach_hops = min(cycle_size - 1, (cycle_size * length // 2 - 1 + length - 1) // length)

    pair_blocks = [keyvals[0]]
    label_blocks = [documents[0]]
    place_blocks = [position * length + offsets]
    label_slab = jnp.broadcast_to(
        documents[0].astype(jnp.bfloat16)[:, None, None], (length, 1, pair_width)
    )
    packed = jnp.concatenate([keyvals[0], label_slab], axis=1)
    for hop in range(1, reach_hops + 1):
        arrived = shifted(packed, "ctx", hop)
        pair_blocks.append(arrived[:, :2])
        label_blocks.append(arrived[:, 2, 0].astype(jnp.int32))
        place_blocks.append((position - hop) * length + offsets)
    pairs = jnp.concatenate(pair_blocks, axis=0)
    key_labels = jnp.concatenate(label_blocks, axis=0)
    key_place = jnp.concatenate(place_blocks, axis=0)
    key_count = pairs.shape[0]

    query_place = position * length + offsets
    query_labels = documents[0]
    query_block = queries[0].reshape(length, pair_heads, query_group_size, HEAD_DIM)
    key_block = pairs[:, 0].reshape(key_count, pair_heads, HEAD_DIM)
    value_block = pairs[:, 1].reshape(key_count, pair_heads, HEAD_DIM)

    scores = jnp.einsum(
        "qhgd,khd->hgqk", query_block, key_block, preferred_element_type=jnp.float32
    )
    scores = scores * (1.0 / math.sqrt(HEAD_DIM))
    allowed = (
        (query_labels[:, None] == key_labels[None, :])
        & (key_place[None, :] <= query_place[:, None])
        & (key_place[None, :] >= 0)
    )
    scores = jnp.where(allowed, scores, FLOOR_SCORE)
    peak = jnp.max(scores, axis=-1, keepdims=True)
    expo = jnp.where(allowed, jnp.exp(scores - peak), 0.0)
    total = jnp.sum(expo, axis=-1)
    summed = jnp.einsum(
        "hgqk,khd->qhgd",
        expo.astype(jnp.bfloat16),
        value_block,
        preferred_element_type=jnp.float32,
    )
    head_values = summed / jnp.transpose(total, (2, 0, 1))[..., None]
    return head_values.reshape(length, pair_heads * query_group_size * HEAD_DIM).astype(
        jnp.bfloat16
    )


def swapped(block, axis):
    return lax.ppermute(block, axis, [(0, 1), (1, 0)])


def sent(block, route):
    return lax.ppermute(block, ("dp", "tensor"), route)


def needed_heads(head_values):
    group = lax.axis_size("tensor")
    me = lax.axis_index("tensor")
    side = lax.axis_index("dp")
    foreign = swapped(head_values, "dp")
    mine = jnp.concatenate([head_values, foreign], axis=1)
    owners = [(s, 2 * s + k) for s in range(2) for k in range(2)]
    over_y = sent(mine, [(s * group + p, s * group + (p ^ 2)) for s, p in owners])
    beside = sent(mine, [(s * group + p, s * group + (p ^ 1)) for s, p in owners])
    relayed = sent(
        over_y, [(s * group + (p ^ 2), s * group + (p ^ 3)) for s, p in owners]
    )
    on_owner = me // 2 == side
    same_core = jnp.where(on_owner, mine, over_y)
    other_core = jnp.where(on_owner, beside, relayed)
    first_core = me % 2 == 0
    return [
        jnp.where(first_core, same_core, other_core),
        jnp.where(first_core, other_core, same_core),
    ]


def split_projection(head_values, output_weight):
    width = head_values.shape[1]
    columns = output_weight.shape[1]
    half = columns // 2
    side_rows = [
        lax.all_gather(output_weight[:, :half], "ctx", axis=0, tiled=True),
        lax.all_gather(output_weight[:, half:], "ctx", axis=0, tiled=True),
    ]
    peers = needed_heads(head_values)
    outputs = []
    for rows in side_rows:
        local = None
        partner = None
        for j, both in enumerate(peers):
            block = rows[j * width:(j + 1) * width]
            mine = jnp.dot(both[:, :width], block, preferred_element_type=jnp.float32)
            theirs = jnp.dot(both[:, width:], block, preferred_element_type=jnp.float32)
            local = mine if local is None else local + mine
            partner = theirs if partner is None else partner + theirs
        returned = swapped(partner.astype(jnp.bfloat16), "dp")
        outputs.append(local + returned.astype(jnp.float32))
    return jnp.concatenate(outputs, axis=1)


def shards(queries, keyvals, documents, output_weight):
    block_rows = output_weight.shape[0]
    width = queries.shape[2]
    side_width = block_rows * lax.axis_size("ctx")
    fits = output_weight.shape[1] % 256 == 0 and lax.axis_size("tensor") == 4
    if lax.axis_size("dp") == 2 and side_width == 2 * width and fits:
        head_values = attention(queries, keyvals, documents)
        result = split_projection(head_values, output_weight)
        return result.astype(jnp.bfloat16)[None]
    all_rows = lax.all_gather(output_weight, ("dp", "ctx"), axis=0, tiled=True)
    head_values = attention(queries, keyvals, documents)
    group = lax.axis_size("tensor")
    me = lax.axis_index("tensor")
    result = None
    for distance in range(group):
        held = head_values if distance == 0 else rotated(head_values, "tensor", distance)
        owner = (me - distance) % group
        rows = lax.dynamic_slice_in_dim(all_rows, owner * width, width, 0)
        part = jnp.dot(held, rows, preferred_element_type=jnp.float32)
        result = part if result is None else result + part
    return result.astype(jnp.bfloat16)[None]


def solution(mesh):
    placed = (
        P("dp", "ctx", "tensor"),
        P("dp", "ctx", None, "tensor"),
        P("dp", "ctx"),
        P(("dp", "ctx"), "tensor"),
    )
    return jax.shard_map(
        shards, mesh=mesh, in_specs=placed, out_specs=P("dp", "ctx", "tensor"), check_vma=False
    )
```

```python
import math

import jax
import jax.numpy as jnp
from jax import lax
from jax.sharding import PartitionSpec as P

HEAD_DIM = 128


FLOOR_SCORE = -1e30


def shifted(block, axis, distance):
    devices = range(lax.axis_size(axis))
    route = [(i - distance, i) for i in devices if i - distance in devices]
    return lax.ppermute(block, axis, route)


def rotated(block, axis, distance):
    count = lax.axis_size(axis)
    route = [(i, (i + distance) % count) for i in range(count)]
    return lax.ppermute(block, axis, route)


def attention(queries, keyvals, documents):
    length = queries.shape[1]
    pair_width = keyvals.shape[3]
    pair_heads = pair_width // HEAD_DIM
    query_group_size = queries.shape[2] // pair_width
    cycle_size = lax.axis_size("ctx")
    position = lax.axis_index("ctx")
    offsets = jnp.arange(length, dtype=jnp.int32)
    reach_hops = min(cycle_size - 1, (cycle_size * length // 2 - 1 + length - 1) // length)

    pair_blocks = [keyvals[0]]
    label_blocks = [documents[0]]
    place_blocks = [position * length + offsets]
    label_slab = jnp.broadcast_to(
        documents[0].astype(jnp.bfloat16)[:, None, None], (length, 1, pair_width)
    )
    packed = jnp.concatenate([keyvals[0], label_slab], axis=1)
    for hop in range(1, reach_hops + 1):
        arrived = shifted(packed, "ctx", hop)
        pair_blocks.append(arrived[:, :2])
        label_blocks.append(arrived[:, 2, 0].astype(jnp.int32))
        place_blocks.append((position - hop) * length + offsets)
    pairs = jnp.concatenate(pair_blocks, axis=0)
    key_labels = jnp.concatenate(label_blocks, axis=0)
    key_place = jnp.concatenate(place_blocks, axis=0)
    key_count = pairs.shape[0]

    query_place = position * length + offsets
    query_labels = documents[0]
    query_block = queries[0].reshape(length, pair_heads, query_group_size, HEAD_DIM)
    key_block = pairs[:, 0].reshape(key_count, pair_heads, HEAD_DIM)
    value_block = pairs[:, 1].reshape(key_count, pair_heads, HEAD_DIM)

    scores = jnp.einsum(
        "qhgd,khd->hgqk", query_block, key_block, preferred_element_type=jnp.float32
    )
    scores = scores * (1.0 / math.sqrt(HEAD_DIM))
    allowed = (
        (query_labels[:, None] == key_labels[None, :])
        & (key_place[None, :] <= query_place[:, None])
        & (key_place[None, :] >= 0)
    )
    scores = jnp.where(allowed, scores, FLOOR_SCORE)
    peak = jnp.max(scores, axis=-1, keepdims=True)
    expo = jnp.where(allowed, jnp.exp(scores - peak), 0.0)
    total = jnp.sum(expo, axis=-1)
    summed = jnp.einsum(
        "hgqk,khd->qhgd",
        expo.astype(jnp.bfloat16),
        value_block,
        preferred_element_type=jnp.float32,
    )
    head_values = summed / jnp.transpose(total, (2, 0, 1))[..., None]
    return head_values.reshape(length, pair_heads * query_group_size * HEAD_DIM).astype(
        jnp.bfloat16
    )


def swapped(block, axis):
    return lax.ppermute(block, axis, [(0, 1), (1, 0)])


def sent(block, route):
    return lax.ppermute(block, ("dp", "tensor"), route)


def needed_heads(head_values):
    group = lax.axis_size("tensor")
    me = lax.axis_index("tensor")
    side = lax.axis_index("dp")
    foreign = swapped(head_values, "dp")
    mine = jnp.concatenate([head_values, foreign], axis=1)
    owners = [(s, 2 * s + k) for s in range(2) for k in range(2)]
    over_y = sent(mine, [(s * group + p, s * group + (p ^ 2)) for s, p in owners])
    beside = sent(mine, [(s * group + p, s * group + (p ^ 1)) for s, p in owners])
    relayed = sent(
        over_y, [(s * group + (p ^ 2), s * group + (p ^ 3)) for s, p in owners]
    )
    on_owner = me // 2 == side
    same_core = jnp.where(on_owner, mine, over_y)
    other_core = jnp.where(on_owner, beside, relayed)
    first_core = me % 2 == 0
    return [
        jnp.where(first_core, same_core, other_core),
        jnp.where(first_core, other_core, same_core),
    ]


def split_projection(head_values, side_rows):
    width = head_values.shape[1]
    peers = needed_heads(head_values)
    local = None
    partner = None
    for j, both in enumerate(peers):
        block = side_rows[j * width:(j + 1) * width]
        mine = jnp.dot(both[:, :width], block, preferred_element_type=jnp.float32)
        theirs = jnp.dot(both[:, width:], block, preferred_element_type=jnp.float32)
        local = mine if local is None else local + mine
        partner = theirs if partner is None else partner + theirs
    returned = swapped(partner.astype(jnp.bfloat16), "dp")
    return local + returned.astype(jnp.float32)


def shards(queries, keyvals, documents, output_weight):
    block_rows = output_weight.shape[0]
    width = queries.shape[2]
    side_width = block_rows * lax.axis_size("ctx")
    fits = lax.axis_size("tensor") == 4
    if lax.axis_size("dp") == 2 and side_width == 2 * width and fits:
        side_rows = lax.all_gather(output_weight, "ctx", axis=0, tiled=True)
        head_values = attention(queries, keyvals, documents)
        result = split_projection(head_values, side_rows)
        return result.astype(jnp.bfloat16)[None]
    all_rows = lax.all_gather(output_weight, ("dp", "ctx"), axis=0, tiled=True)
    head_values = attention(queries, keyvals, documents)
    group = lax.axis_size("tensor")
    me = lax.axis_index("tensor")
    result = None
    for distance in range(group):
        held = head_values if distance == 0 else rotated(head_values, "tensor", distance)
        owner = (me - distance) % group
        rows = lax.dynamic_slice_in_dim(all_rows, owner * width, width, 0)
        part = jnp.dot(held, rows, preferred_element_type=jnp.float32)
        result = part if result is None else result + part
    return result.astype(jnp.bfloat16)[None]


def solution(mesh):
    placed = (
        P("dp", "ctx", "tensor"),
        P("dp", "ctx", None, "tensor"),
        P("dp", "ctx"),
        P(("dp", "ctx"), "tensor"),
    )
    return jax.shard_map(
        shards, mesh=mesh, in_specs=placed, out_specs=P("dp", "ctx", "tensor"), check_vma=False
    )
```

```python
import math

import jax
import jax.numpy as jnp
from jax import lax
from jax.sharding import PartitionSpec as P

HEAD_DIM = 128


FLOOR_SCORE = -1e30


def shifted(block, axis, distance):
    devices = range(lax.axis_size(axis))
    route = [(i - distance, i) for i in devices if i - distance in devices]
    return lax.ppermute(block, axis, route)


def rotated(block, axis, distance):
    count = lax.axis_size(axis)
    route = [(i, (i + distance) % count) for i in range(count)]
    return lax.ppermute(block, axis, route)


def attention(queries, keyvals, documents):
    length = queries.shape[1]
    pair_width = keyvals.shape[3]
    pair_heads = pair_width // HEAD_DIM
    query_group_size = queries.shape[2] // pair_width
    cycle_size = lax.axis_size("ctx")
    position = lax.axis_index("ctx")
    offsets = jnp.arange(length, dtype=jnp.int32)
    reach_hops = min(cycle_size - 1, (cycle_size * length // 2 - 1 + length - 1) // length)

    pair_blocks = [keyvals[0]]
    label_blocks = [documents[0]]
    place_blocks = [position * length + offsets]
    label_slab = jnp.broadcast_to(
        documents[0].astype(jnp.bfloat16)[:, None, None], (length, 1, pair_width)
    )
    packed = jnp.concatenate([keyvals[0], label_slab], axis=1)
    for hop in range(1, reach_hops + 1):
        arrived = shifted(packed, "ctx", hop)
        pair_blocks.append(arrived[:, :2])
        label_blocks.append(arrived[:, 2, 0].astype(jnp.int32))
        place_blocks.append((position - hop) * length + offsets)
    pairs = jnp.concatenate(pair_blocks, axis=0)
    key_labels = jnp.concatenate(label_blocks, axis=0)
    key_place = jnp.concatenate(place_blocks, axis=0)
    key_count = pairs.shape[0]

    query_place = position * length + offsets
    query_labels = documents[0]
    query_block = queries[0].reshape(length, pair_heads, query_group_size, HEAD_DIM)
    key_block = pairs[:, 0].reshape(key_count, pair_heads, HEAD_DIM)
    value_block = pairs[:, 1].reshape(key_count, pair_heads, HEAD_DIM)

    scores = jnp.einsum(
        "qhgd,khd->hgqk", query_block, key_block, preferred_element_type=jnp.float32
    )
    scores = scores * (1.0 / math.sqrt(HEAD_DIM))
    allowed = (
        (query_labels[:, None] == key_labels[None, :])
        & (key_place[None, :] <= query_place[:, None])
        & (key_place[None, :] >= 0)
    )
    scores = jnp.where(allowed, scores, FLOOR_SCORE)
    peak = jnp.max(scores, axis=-1, keepdims=True)
    expo = jnp.where(allowed, jnp.exp(scores - peak), 0.0)
    total = jnp.sum(expo, axis=-1)
    summed = jnp.einsum(
        "hgqk,khd->qhgd",
        expo.astype(jnp.bfloat16),
        value_block,
        preferred_element_type=jnp.float32,
    )
    head_values = summed / jnp.transpose(total, (2, 0, 1))[..., None]
    return head_values.reshape(length, pair_heads * query_group_size * HEAD_DIM).astype(
        jnp.bfloat16
    )


def swapped(block, axis):
    return lax.ppermute(block, axis, [(0, 1), (1, 0)])


def sent(block, route):
    return lax.ppermute(block, ("dp", "tensor"), route)


def needed_heads(head_values):
    group = lax.axis_size("tensor")
    me = lax.axis_index("tensor")
    side = lax.axis_index("dp")
    foreign = swapped(head_values, "dp")
    mine = jnp.concatenate([head_values, foreign], axis=1)
    owners = [(s, 2 * s + k) for s in range(2) for k in range(2)]
    over_y = sent(mine, [(s * group + p, s * group + (p ^ 2)) for s, p in owners])
    beside = sent(mine, [(s * group + p, s * group + (p ^ 1)) for s, p in owners])
    relayed = sent(
        over_y, [(s * group + (p ^ 2), s * group + (p ^ 3)) for s, p in owners]
    )
    on_owner = me // 2 == side
    same_core = jnp.where(on_owner, mine, over_y)
    other_core = jnp.where(on_owner, beside, relayed)
    first_core = me % 2 == 0
    return [
        jnp.where(first_core, same_core, other_core),
        jnp.where(first_core, other_core, same_core),
    ]


def split_projection(head_values, side_rows):
    width = head_values.shape[1]
    peers = needed_heads(head_values)
    partner = None
    for j, both in enumerate(peers):
        block = side_rows[j * width:(j + 1) * width]
        theirs = jnp.dot(both[:, width:], block, preferred_element_type=jnp.float32)
        partner = theirs if partner is None else partner + theirs
    outgoing = partner.astype(jnp.bfloat16)
    returned = swapped(outgoing, "dp")
    outgoing, peers, side_rows = lax.optimization_barrier((outgoing, peers, side_rows))
    local = None
    for j, both in enumerate(peers):
        block = side_rows[j * width:(j + 1) * width]
        mine = jnp.dot(both[:, :width], block, preferred_element_type=jnp.float32)
        local = mine if local is None else local + mine
    return local + returned.astype(jnp.float32)


def shards(queries, keyvals, documents, output_weight):
    block_rows = output_weight.shape[0]
    width = queries.shape[2]
    side_width = block_rows * lax.axis_size("ctx")
    fits = lax.axis_size("tensor") == 4
    if lax.axis_size("dp") == 2 and side_width == 2 * width and fits:
        side_rows = lax.all_gather(output_weight, "ctx", axis=0, tiled=True)
        head_values = attention(queries, keyvals, documents)
        result = split_projection(head_values, side_rows)
        return result.astype(jnp.bfloat16)[None]
    all_rows = lax.all_gather(output_weight, ("dp", "ctx"), axis=0, tiled=True)
    head_values = attention(queries, keyvals, documents)
    group = lax.axis_size("tensor")
    me = lax.axis_index("tensor")
    result = None
    for distance in range(group):
        held = head_values if distance == 0 else rotated(head_values, "tensor", distance)
        owner = (me - distance) % group
        rows = lax.dynamic_slice_in_dim(all_rows, owner * width, width, 0)
        part = jnp.dot(held, rows, preferred_element_type=jnp.float32)
        result = part if result is None else result + part
    return result.astype(jnp.bfloat16)[None]


def solution(mesh):
    placed = (
        P("dp", "ctx", "tensor"),
        P("dp", "ctx", None, "tensor"),
        P("dp", "ctx"),
        P(("dp", "ctx"), "tensor"),
    )
    return jax.shard_map(
        shards, mesh=mesh, in_specs=placed, out_specs=P("dp", "ctx", "tensor"), check_vma=False
    )
```

```python
import math

import jax
import jax.numpy as jnp
from jax import lax
from jax.sharding import PartitionSpec as P

HEAD_DIM = 128


FLOOR_SCORE = -1e30


def shifted(block, axis, distance):
    devices = range(lax.axis_size(axis))
    route = [(i - distance, i) for i in devices if i - distance in devices]
    return lax.ppermute(block, axis, route)


def rotated(block, axis, distance):
    count = lax.axis_size(axis)
    route = [(i, (i + distance) % count) for i in range(count)]
    return lax.ppermute(block, axis, route)


def attention(queries, keyvals, documents):
    length = queries.shape[1]
    pair_width = keyvals.shape[3]
    pair_heads = pair_width // HEAD_DIM
    query_group_size = queries.shape[2] // pair_width
    cycle_size = lax.axis_size("ctx")
    position = lax.axis_index("ctx")
    offsets = jnp.arange(length, dtype=jnp.int32)
    reach_hops = min(cycle_size - 1, (cycle_size * length // 2 - 1 + length - 1) // length)

    pair_blocks = [keyvals[0]]
    label_blocks = [documents[0]]
    place_blocks = [position * length + offsets]
    label_slab = jnp.broadcast_to(
        documents[0].astype(jnp.bfloat16)[:, None, None], (length, 1, pair_width)
    )
    packed = jnp.concatenate([keyvals[0], label_slab], axis=1)
    for hop in range(1, reach_hops + 1):
        arrived = shifted(packed, "ctx", hop)
        pair_blocks.append(arrived[:, :2])
        label_blocks.append(arrived[:, 2, 0].astype(jnp.int32))
        place_blocks.append((position - hop) * length + offsets)
    pairs = jnp.concatenate(pair_blocks, axis=0)
    key_labels = jnp.concatenate(label_blocks, axis=0)
    key_place = jnp.concatenate(place_blocks, axis=0)
    key_count = pairs.shape[0]

    query_place = position * length + offsets
    query_labels = documents[0]
    query_block = queries[0].reshape(length, pair_heads, query_group_size, HEAD_DIM)
    key_block = pairs[:, 0].reshape(key_count, pair_heads, HEAD_DIM)
    value_block = pairs[:, 1].reshape(key_count, pair_heads, HEAD_DIM)

    scores = jnp.einsum(
        "qhgd,khd->hgqk", query_block, key_block, preferred_element_type=jnp.float32
    )
    scores = scores * (1.0 / math.sqrt(HEAD_DIM))
    allowed = (
        (query_labels[:, None] == key_labels[None, :])
        & (key_place[None, :] <= query_place[:, None])
        & (key_place[None, :] >= 0)
    )
    scores = jnp.where(allowed, scores, FLOOR_SCORE)
    peak = jnp.max(scores, axis=-1, keepdims=True)
    expo = jnp.where(allowed, jnp.exp(scores - peak), 0.0)
    total = jnp.sum(expo, axis=-1)
    summed = jnp.einsum(
        "hgqk,khd->qhgd",
        expo.astype(jnp.bfloat16),
        value_block,
        preferred_element_type=jnp.float32,
    )
    head_values = summed / jnp.transpose(total, (2, 0, 1))[..., None]
    return head_values.reshape(length, pair_heads * query_group_size * HEAD_DIM).astype(
        jnp.bfloat16
    )


def swapped(block, axis):
    return lax.ppermute(block, axis, [(0, 1), (1, 0)])


def sent(block, route):
    return lax.ppermute(block, ("dp", "tensor"), route)


def needed_heads(head_values):
    group = lax.axis_size("tensor")
    me = lax.axis_index("tensor")
    side = lax.axis_index("dp")
    foreign = swapped(head_values, "dp")
    mine = jnp.concatenate([head_values, foreign], axis=1)
    owners = [(s, 2 * s + k) for s in range(2) for k in range(2)]
    over_y = sent(mine, [(s * group + p, s * group + (p ^ 2)) for s, p in owners])
    beside = sent(mine, [(s * group + p, s * group + (p ^ 1)) for s, p in owners])
    relayed = sent(
        over_y, [(s * group + (p ^ 2), s * group + (p ^ 3)) for s, p in owners]
    )
    on_owner = me // 2 == side
    same_core = jnp.where(on_owner, mine, over_y)
    other_core = jnp.where(on_owner, beside, relayed)
    first_core = me % 2 == 0
    width = head_values.shape[1]
    lower = jnp.where(first_core, same_core, other_core)
    upper = jnp.where(first_core, other_core, same_core)
    own_full = jnp.concatenate([lower[:, :width], upper[:, :width]], axis=1)
    foreign_full = jnp.concatenate([lower[:, width:], upper[:, width:]], axis=1)
    return own_full, foreign_full


def split_projection(head_values, side_rows):
    own_full, foreign_full = needed_heads(head_values)
    partner = jnp.dot(foreign_full, side_rows, preferred_element_type=jnp.float32)
    outgoing = partner.astype(jnp.bfloat16)
    returned = swapped(outgoing, "dp")
    outgoing, own_full, side_rows = lax.optimization_barrier((outgoing, own_full, side_rows))
    local = jnp.dot(own_full, side_rows, preferred_element_type=jnp.float32)
    local = lax.optimization_barrier(local)
    return local + returned.astype(jnp.float32)


def shards(queries, keyvals, documents, output_weight):
    block_rows = output_weight.shape[0]
    width = queries.shape[2]
    side_width = block_rows * lax.axis_size("ctx")
    fits = lax.axis_size("tensor") == 4
    if lax.axis_size("dp") == 2 and side_width == 2 * width and fits:
        side_rows = lax.all_gather(output_weight, "ctx", axis=0, tiled=True)
        head_values = attention(queries, keyvals, documents)
        result = split_projection(head_values, side_rows)
        return result.astype(jnp.bfloat16)[None]
    all_rows = lax.all_gather(output_weight, ("dp", "ctx"), axis=0, tiled=True)
    head_values = attention(queries, keyvals, documents)
    group = lax.axis_size("tensor")
    me = lax.axis_index("tensor")
    result = None
    for distance in range(group):
        held = head_values if distance == 0 else rotated(head_values, "tensor", distance)
        owner = (me - distance) % group
        rows = lax.dynamic_slice_in_dim(all_rows, owner * width, width, 0)
        part = jnp.dot(held, rows, preferred_element_type=jnp.float32)
        result = part if result is None else result + part
    return result.astype(jnp.bfloat16)[None]


def solution(mesh):
    placed = (
        P("dp", "ctx", "tensor"),
        P("dp", "ctx", None, "tensor"),
        P("dp", "ctx"),
        P(("dp", "ctx"), "tensor"),
    )
    return jax.shard_map(
        shards, mesh=mesh, in_specs=placed, out_specs=P("dp", "ctx", "tensor"), check_vma=False
    )
```

```python
import math

import jax
import jax.numpy as jnp
from jax import lax
from jax.sharding import PartitionSpec as P

HEAD_DIM = 128


FLOOR_SCORE = -1e30


def shifted(block, axis, distance):
    devices = range(lax.axis_size(axis))
    route = [(i - distance, i) for i in devices if i - distance in devices]
    return lax.ppermute(block, axis, route)


def rotated(block, axis, distance):
    count = lax.axis_size(axis)
    route = [(i, (i + distance) % count) for i in range(count)]
    return lax.ppermute(block, axis, route)


def attention(queries, keyvals, documents):
    length = queries.shape[1]
    pair_width = keyvals.shape[3]
    pair_heads = pair_width // HEAD_DIM
    query_group_size = queries.shape[2] // pair_width
    cycle_size = lax.axis_size("ctx")
    position = lax.axis_index("ctx")
    offsets = jnp.arange(length, dtype=jnp.int32)
    reach_hops = min(cycle_size - 1, (cycle_size * length // 2 - 1 + length - 1) // length)

    pair_blocks = [keyvals[0]]
    label_blocks = [documents[0]]
    place_blocks = [position * length + offsets]
    label_slab = jnp.broadcast_to(
        documents[0].astype(jnp.bfloat16)[:, None, None], (length, 1, pair_width)
    )
    packed = jnp.concatenate([keyvals[0], label_slab], axis=1)
    for hop in range(1, reach_hops + 1):
        arrived = shifted(packed, "ctx", hop)
        pair_blocks.append(arrived[:, :2])
        label_blocks.append(arrived[:, 2, 0].astype(jnp.int32))
        place_blocks.append((position - hop) * length + offsets)
    pairs = jnp.concatenate(pair_blocks, axis=0)
    key_labels = jnp.concatenate(label_blocks, axis=0)
    key_place = jnp.concatenate(place_blocks, axis=0)
    key_count = pairs.shape[0]

    query_place = position * length + offsets
    query_labels = documents[0]
    query_block = queries[0].reshape(length, pair_heads, query_group_size, HEAD_DIM)
    key_block = pairs[:, 0].reshape(key_count, pair_heads, HEAD_DIM)
    value_block = pairs[:, 1].reshape(key_count, pair_heads, HEAD_DIM)

    scores = jnp.einsum(
        "qhgd,khd->hgqk", query_block, key_block, preferred_element_type=jnp.float32
    )
    scores = scores * (1.0 / math.sqrt(HEAD_DIM))
    allowed = (
        (query_labels[:, None] == key_labels[None, :])
        & (key_place[None, :] <= query_place[:, None])
        & (key_place[None, :] >= 0)
    )
    scores = jnp.where(allowed, scores, FLOOR_SCORE)
    peak = jnp.max(scores, axis=-1, keepdims=True)
    expo = jnp.where(allowed, jnp.exp(scores - peak), 0.0)
    total = jnp.sum(expo, axis=-1)
    summed = jnp.einsum(
        "hgqk,khd->qhgd",
        expo.astype(jnp.bfloat16),
        value_block,
        preferred_element_type=jnp.float32,
    )
    head_values = summed / jnp.transpose(total, (2, 0, 1))[..., None]
    return head_values.reshape(length, pair_heads * query_group_size * HEAD_DIM).astype(
        jnp.bfloat16
    )


def swapped(block, axis):
    return lax.ppermute(block, axis, [(0, 1), (1, 0)])


def sent(block, route):
    return lax.ppermute(block, ("dp", "tensor"), route)


def needed_heads(head_values):
    group = lax.axis_size("tensor")
    me = lax.axis_index("tensor")
    side = lax.axis_index("dp")
    foreign = swapped(head_values, "dp")
    mine = jnp.concatenate([head_values, foreign], axis=1)
    owners = [(s, 2 * s + k) for s in range(2) for k in range(2)]
    over_y = sent(mine, [(s * group + p, s * group + (p ^ 2)) for s, p in owners])
    beside = sent(mine, [(s * group + p, s * group + (p ^ 1)) for s, p in owners])
    relayed = sent(
        over_y, [(s * group + (p ^ 2), s * group + (p ^ 3)) for s, p in owners]
    )
    on_owner = me // 2 == side
    same_core = jnp.where(on_owner, mine, over_y)
    other_core = jnp.where(on_owner, beside, relayed)
    first_core = me % 2 == 0
    width = head_values.shape[1]
    lower = jnp.where(first_core, same_core, other_core)
    upper = jnp.where(first_core, other_core, same_core)
    own_full = jnp.concatenate([lower[:, :width], upper[:, :width]], axis=1)
    foreign_full = jnp.concatenate([lower[:, width:], upper[:, width:]], axis=1)
    return own_full, foreign_full


def line_blocks(block, axis):
    count = lax.axis_size(axis)
    here = lax.axis_index(axis)
    blocks = [(block, here)]
    rising, falling = block, block
    for step in range(1, count):
        rising = lax.ppermute(rising, axis, [(i, i + 1) for i in range(step - 1, count - 1)])
        falling = lax.ppermute(falling, axis, [(i, i - 1) for i in range(1, count - step + 1)])
        blocks.append((rising, jnp.clip(here - step, 0, count - 1)))
        blocks.append((falling, jnp.clip(here + step, 0, count - 1)))
    return blocks


def blockwise(heads, blocks, block_rows):
    total = None
    for block, row_block in blocks:
        columns = lax.dynamic_slice_in_dim(heads, row_block * block_rows, block_rows, 1)
        part = jnp.dot(columns, block, preferred_element_type=jnp.float32)
        total = part if total is None else total + part
    return total


def split_projection(head_values, chained):
    block_rows = chained[0][0].shape[0]
    own_full, foreign_full = needed_heads(head_values)
    outgoing = blockwise(foreign_full, chained, block_rows).astype(jnp.bfloat16)
    returned = swapped(outgoing, "dp")
    outgoing, own_full, chained = lax.optimization_barrier((outgoing, own_full, chained))
    local = lax.optimization_barrier(blockwise(own_full, chained, block_rows))
    return local + returned.astype(jnp.float32)


def shards(queries, keyvals, documents, output_weight):
    block_rows = output_weight.shape[0]
    width = queries.shape[2]
    side_width = block_rows * lax.axis_size("ctx")
    fits = lax.axis_size("tensor") == 4
    if lax.axis_size("dp") == 2 and side_width == 2 * width and fits:
        chained = line_blocks(output_weight, "ctx")
        head_values = attention(queries, keyvals, documents)
        result = split_projection(head_values, chained)
        return result.astype(jnp.bfloat16)[None]
    all_rows = lax.all_gather(output_weight, ("dp", "ctx"), axis=0, tiled=True)
    head_values = attention(queries, keyvals, documents)
    group = lax.axis_size("tensor")
    me = lax.axis_index("tensor")
    result = None
    for distance in range(group):
        held = head_values if distance == 0 else rotated(head_values, "tensor", distance)
        owner = (me - distance) % group
        rows = lax.dynamic_slice_in_dim(all_rows, owner * width, width, 0)
        part = jnp.dot(held, rows, preferred_element_type=jnp.float32)
        result = part if result is None else result + part
    return result.astype(jnp.bfloat16)[None]


def solution(mesh):
    placed = (
        P("dp", "ctx", "tensor"),
        P("dp", "ctx", None, "tensor"),
        P("dp", "ctx"),
        P(("dp", "ctx"), "tensor"),
    )
    return jax.shard_map(
        shards, mesh=mesh, in_specs=placed, out_specs=P("dp", "ctx", "tensor"), check_vma=False
    )
```

```python
import math

import jax
import jax.numpy as jnp
from jax import lax
from jax.sharding import PartitionSpec as P

HEAD_DIM = 128


FLOOR_SCORE = -1e30


def shifted(block, axis, distance):
    devices = range(lax.axis_size(axis))
    route = [(i - distance, i) for i in devices if i - distance in devices]
    return lax.ppermute(block, axis, route)


def rotated(block, axis, distance):
    count = lax.axis_size(axis)
    route = [(i, (i + distance) % count) for i in range(count)]
    return lax.ppermute(block, axis, route)


def attention(queries, keyvals, documents):
    length = queries.shape[1]
    pair_width = keyvals.shape[3]
    pair_heads = pair_width // HEAD_DIM
    query_group_size = queries.shape[2] // pair_width
    cycle_size = lax.axis_size("ctx")
    position = lax.axis_index("ctx")
    offsets = jnp.arange(length, dtype=jnp.int32)
    reach_hops = min(cycle_size - 1, (cycle_size * length // 2 - 1 + length - 1) // length)

    pair_blocks = [keyvals[0]]
    label_blocks = [documents[0]]
    place_blocks = [position * length + offsets]
    label_slab = jnp.broadcast_to(
        documents[0].astype(jnp.bfloat16)[:, None, None], (length, 1, pair_width)
    )
    packed = jnp.concatenate([keyvals[0], label_slab], axis=1)
    for hop in range(1, reach_hops + 1):
        arrived = shifted(packed, "ctx", hop)
        pair_blocks.append(arrived[:, :2])
        label_blocks.append(arrived[:, 2, 0].astype(jnp.int32))
        place_blocks.append((position - hop) * length + offsets)
    pairs = jnp.concatenate(pair_blocks, axis=0)
    key_labels = jnp.concatenate(label_blocks, axis=0)
    key_place = jnp.concatenate(place_blocks, axis=0)
    key_count = pairs.shape[0]

    query_place = position * length + offsets
    query_labels = documents[0]
    query_block = queries[0].reshape(length, pair_heads, query_group_size, HEAD_DIM)
    key_block = pairs[:, 0].reshape(key_count, pair_heads, HEAD_DIM)
    value_block = pairs[:, 1].reshape(key_count, pair_heads, HEAD_DIM)

    scores = jnp.einsum(
        "qhgd,khd->hgqk", query_block, key_block, preferred_element_type=jnp.float32
    )
    scores = scores * (1.0 / math.sqrt(HEAD_DIM))
    allowed = (
        (query_labels[:, None] == key_labels[None, :])
        & (key_place[None, :] <= query_place[:, None])
        & (key_place[None, :] >= 0)
    )
    scores = jnp.where(allowed, scores, FLOOR_SCORE)
    peak = jnp.max(scores, axis=-1, keepdims=True)
    expo = jnp.where(allowed, jnp.exp(scores - peak), 0.0)
    total = jnp.sum(expo, axis=-1)
    summed = jnp.einsum(
        "hgqk,khd->qhgd",
        expo.astype(jnp.bfloat16),
        value_block,
        preferred_element_type=jnp.float32,
    )
    head_values = summed / jnp.transpose(total, (2, 0, 1))[..., None]
    return head_values.reshape(length, pair_heads * query_group_size * HEAD_DIM).astype(
        jnp.bfloat16
    )


def swapped(block, axis):
    return lax.ppermute(block, axis, [(0, 1), (1, 0)])


def sent(block, route):
    return lax.ppermute(block, ("dp", "tensor"), route)


def needed_heads(head_values):
    group = lax.axis_size("tensor")
    me = lax.axis_index("tensor")
    side = lax.axis_index("dp")
    foreign = swapped(head_values, "dp")
    mine = jnp.concatenate([head_values, foreign], axis=1)
    owners = [(s, 2 * s + k) for s in range(2) for k in range(2)]
    over_y = sent(mine, [(s * group + p, s * group + (p ^ 2)) for s, p in owners])
    beside = sent(mine, [(s * group + p, s * group + (p ^ 1)) for s, p in owners])
    relayed = sent(
        over_y, [(s * group + (p ^ 2), s * group + (p ^ 3)) for s, p in owners]
    )
    on_owner = me // 2 == side
    same_core = jnp.where(on_owner, mine, over_y)
    other_core = jnp.where(on_owner, beside, relayed)
    first_core = me % 2 == 0
    width = head_values.shape[1]
    lower = jnp.where(first_core, same_core, other_core)
    upper = jnp.where(first_core, other_core, same_core)
    own_full = jnp.concatenate([lower[:, :width], upper[:, :width]], axis=1)
    foreign_full = jnp.concatenate([lower[:, width:], upper[:, width:]], axis=1)
    return own_full, foreign_full


def line_rows(block, axis):
    count = lax.axis_size(axis)
    here = lax.axis_index(axis)
    arrivals = [(block, 0)]
    rising, falling = block, block
    for step in range(1, count):
        rising = lax.ppermute(rising, axis, [(i, i + 1) for i in range(step - 1, count - 1)])
        falling = lax.ppermute(falling, axis, [(i, i - 1) for i in range(1, count - step + 1)])
        arrivals.append((rising, -step))
        arrivals.append((falling, step))
    ordered = []
    for place in range(count):
        chosen = jnp.zeros_like(block)
        for arrived, offset in arrivals:
            chosen = jnp.where(here + offset == place, arrived, chosen)
        ordered.append(chosen)
    return jnp.concatenate(ordered, axis=0)


def split_projection(head_values, side_rows):
    own_full, foreign_full = needed_heads(head_values)
    partner = jnp.dot(foreign_full, side_rows, preferred_element_type=jnp.float32)
    outgoing = partner.astype(jnp.bfloat16)
    returned = swapped(outgoing, "dp")
    outgoing, own_full, side_rows = lax.optimization_barrier((outgoing, own_full, side_rows))
    local = jnp.dot(own_full, side_rows, preferred_element_type=jnp.float32)
    local = lax.optimization_barrier(local)
    return local + returned.astype(jnp.float32)


def shards(queries, keyvals, documents, output_weight):
    block_rows = output_weight.shape[0]
    width = queries.shape[2]
    side_width = block_rows * lax.axis_size("ctx")
    fits = lax.axis_size("tensor") == 4
    if lax.axis_size("dp") == 2 and side_width == 2 * width and fits:
        side_rows = line_rows(output_weight, "ctx")
        head_values = attention(queries, keyvals, documents)
        result = split_projection(head_values, side_rows)
        return result.astype(jnp.bfloat16)[None]
    all_rows = lax.all_gather(output_weight, ("dp", "ctx"), axis=0, tiled=True)
    head_values = attention(queries, keyvals, documents)
    group = lax.axis_size("tensor")
    me = lax.axis_index("tensor")
    result = None
    for distance in range(group):
        held = head_values if distance == 0 else rotated(head_values, "tensor", distance)
        owner = (me - distance) % group
        rows = lax.dynamic_slice_in_dim(all_rows, owner * width, width, 0)
        part = jnp.dot(held, rows, preferred_element_type=jnp.float32)
        result = part if result is None else result + part
    return result.astype(jnp.bfloat16)[None]


def solution(mesh):
    placed = (
        P("dp", "ctx", "tensor"),
        P("dp", "ctx", None, "tensor"),
        P("dp", "ctx"),
        P(("dp", "ctx"), "tensor"),
    )
    return jax.shard_map(
        shards, mesh=mesh, in_specs=placed, out_specs=P("dp", "ctx", "tensor"), check_vma=False
    )
```

```python
import math

import jax
import jax.numpy as jnp
from jax import lax
from jax.sharding import PartitionSpec as P

HEAD_DIM = 128


FLOOR_SCORE = -1e30


def shifted(block, axis, distance):
    devices = range(lax.axis_size(axis))
    route = [(i - distance, i) for i in devices if i - distance in devices]
    return lax.ppermute(block, axis, route)


def rotated(block, axis, distance):
    count = lax.axis_size(axis)
    route = [(i, (i + distance) % count) for i in range(count)]
    return lax.ppermute(block, axis, route)


def attention(queries, keyvals, documents):
    length = queries.shape[1]
    pair_width = keyvals.shape[3]
    pair_heads = pair_width // HEAD_DIM
    query_group_size = queries.shape[2] // pair_width
    cycle_size = lax.axis_size("ctx")
    position = lax.axis_index("ctx")
    offsets = jnp.arange(length, dtype=jnp.int32)
    reach_hops = min(cycle_size - 1, (cycle_size * length // 2 - 1 + length - 1) // length)

    pair_blocks = [keyvals[0]]
    label_blocks = [documents[0]]
    place_blocks = [position * length + offsets]
    label_slab = jnp.broadcast_to(
        documents[0].astype(jnp.bfloat16)[:, None, None], (length, 1, pair_width)
    )
    packed = jnp.concatenate([keyvals[0], label_slab], axis=1)
    for hop in range(1, reach_hops + 1):
        arrived = shifted(packed, "ctx", hop)
        pair_blocks.append(arrived[:, :2])
        label_blocks.append(arrived[:, 2, 0].astype(jnp.int32))
        place_blocks.append((position - hop) * length + offsets)
    pairs = jnp.concatenate(pair_blocks, axis=0)
    key_labels = jnp.concatenate(label_blocks, axis=0)
    key_place = jnp.concatenate(place_blocks, axis=0)
    key_count = pairs.shape[0]

    query_place = position * length + offsets
    query_labels = documents[0]
    query_block = queries[0].reshape(length, pair_heads, query_group_size, HEAD_DIM)
    key_block = pairs[:, 0].reshape(key_count, pair_heads, HEAD_DIM)
    value_block = pairs[:, 1].reshape(key_count, pair_heads, HEAD_DIM)

    scores = jnp.einsum(
        "qhgd,khd->hgqk", query_block, key_block, preferred_element_type=jnp.float32
    )
    scores = scores * (1.0 / math.sqrt(HEAD_DIM))
    allowed = (
        (query_labels[:, None] == key_labels[None, :])
        & (key_place[None, :] <= query_place[:, None])
        & (key_place[None, :] >= 0)
    )
    scores = jnp.where(allowed, scores, FLOOR_SCORE)
    peak = jnp.max(scores, axis=-1, keepdims=True)
    expo = jnp.where(allowed, jnp.exp(scores - peak), 0.0)
    total = jnp.sum(expo, axis=-1)
    summed = jnp.einsum(
        "hgqk,khd->qhgd",
        expo.astype(jnp.bfloat16),
        value_block,
        preferred_element_type=jnp.float32,
    )
    head_values = summed / jnp.transpose(total, (2, 0, 1))[..., None]
    return head_values.reshape(length, pair_heads * query_group_size * HEAD_DIM).astype(
        jnp.bfloat16
    )


def swapped(block, axis):
    return lax.ppermute(block, axis, [(0, 1), (1, 0)])


def sent(block, route):
    return lax.ppermute(block, ("dp", "tensor"), route)


def needed_heads(head_values):
    group = lax.axis_size("tensor")
    me = lax.axis_index("tensor")
    side = lax.axis_index("dp")
    foreign = swapped(head_values, "dp")
    mine = jnp.concatenate([head_values, foreign], axis=1)
    owners = [(s, 2 * s + k) for s in range(2) for k in range(2)]
    over_y = sent(mine, [(s * group + p, s * group + (p ^ 2)) for s, p in owners])
    beside = sent(mine, [(s * group + p, s * group + (p ^ 1)) for s, p in owners])
    relayed = sent(
        over_y, [(s * group + (p ^ 2), s * group + (p ^ 3)) for s, p in owners]
    )
    on_owner = me // 2 == side
    same_core = jnp.where(on_owner, mine, over_y)
    other_core = jnp.where(on_owner, beside, relayed)
    first_core = me % 2 == 0
    width = head_values.shape[1]
    lower = jnp.where(first_core, same_core, other_core)
    upper = jnp.where(first_core, other_core, same_core)
    own_full = jnp.concatenate([lower[:, :width], upper[:, :width]], axis=1)
    foreign_full = jnp.concatenate([lower[:, width:], upper[:, width:]], axis=1)
    return own_full, foreign_full


def first_hop(block, axis):
    count = lax.axis_size(axis)
    rising = lax.ppermute(block, axis, [(i, i + 1) for i in range(count - 1)])
    falling = lax.ppermute(block, axis, [(i, i - 1) for i in range(1, count)])
    return rising, falling


def line_rows(block, first, axis):
    count = lax.axis_size(axis)
    here = lax.axis_index(axis)
    rising, falling = first
    arrivals = [(block, 0), (rising, -1), (falling, 1)]
    for step in range(2, count):
        rising = lax.ppermute(rising, axis, [(i, i + 1) for i in range(step - 1, count - 1)])
        falling = lax.ppermute(falling, axis, [(i, i - 1) for i in range(1, count - step + 1)])
        arrivals.append((rising, -step))
        arrivals.append((falling, step))
    ordered = []
    for place in range(count):
        chosen = jnp.zeros_like(block)
        for arrived, offset in arrivals:
            chosen = jnp.where(here + offset == place, arrived, chosen)
        ordered.append(chosen)
    return jnp.concatenate(ordered, axis=0)


def split_projection(head_values, side_rows):
    own_full, foreign_full = needed_heads(head_values)
    partner = jnp.dot(foreign_full, side_rows, preferred_element_type=jnp.float32)
    outgoing = partner.astype(jnp.bfloat16)
    returned = swapped(outgoing, "dp")
    outgoing, own_full, side_rows = lax.optimization_barrier((outgoing, own_full, side_rows))
    local = jnp.dot(own_full, side_rows, preferred_element_type=jnp.float32)
    local = lax.optimization_barrier(local)
    return local + returned.astype(jnp.float32)


def shards(queries, keyvals, documents, output_weight):
    block_rows = output_weight.shape[0]
    width = queries.shape[2]
    side_width = block_rows * lax.axis_size("ctx")
    fits = lax.axis_size("tensor") == 4
    if lax.axis_size("dp") == 2 and side_width == 2 * width and fits:
        first = first_hop(output_weight, "ctx")
        head_values = attention(queries, keyvals, documents)
        first, head_values = lax.optimization_barrier((first, head_values))
        side_rows = line_rows(output_weight, first, "ctx")
        result = split_projection(head_values, side_rows)
        return result.astype(jnp.bfloat16)[None]
    all_rows = lax.all_gather(output_weight, ("dp", "ctx"), axis=0, tiled=True)
    head_values = attention(queries, keyvals, documents)
    group = lax.axis_size("tensor")
    me = lax.axis_index("tensor")
    result = None
    for distance in range(group):
        held = head_values if distance == 0 else rotated(head_values, "tensor", distance)
        owner = (me - distance) % group
        rows = lax.dynamic_slice_in_dim(all_rows, owner * width, width, 0)
        part = jnp.dot(held, rows, preferred_element_type=jnp.float32)
        result = part if result is None else result + part
    return result.astype(jnp.bfloat16)[None]


def solution(mesh):
    placed = (
        P("dp", "ctx", "tensor"),
        P("dp", "ctx", None, "tensor"),
        P("dp", "ctx"),
        P(("dp", "ctx"), "tensor"),
    )
    return jax.shard_map(
        shards, mesh=mesh, in_specs=placed, out_specs=P("dp", "ctx", "tensor"), check_vma=False
    )
```

```python
import math

import jax
import jax.numpy as jnp
from jax import lax
from jax.sharding import PartitionSpec as P

HEAD_DIM = 128


FLOOR_SCORE = -1e30


def shifted(block, axis, distance):
    devices = range(lax.axis_size(axis))
    route = [(i - distance, i) for i in devices if i - distance in devices]
    return lax.ppermute(block, axis, route)


def rotated(block, axis, distance):
    count = lax.axis_size(axis)
    route = [(i, (i + distance) % count) for i in range(count)]
    return lax.ppermute(block, axis, route)


def attention(queries, keyvals, documents, anchor):
    length = queries.shape[1]
    pair_width = keyvals.shape[3]
    pair_heads = pair_width // HEAD_DIM
    query_group_size = queries.shape[2] // pair_width
    cycle_size = lax.axis_size("ctx")
    position = lax.axis_index("ctx")
    offsets = jnp.arange(length, dtype=jnp.int32)
    reach_hops = min(cycle_size - 1, (cycle_size * length // 2 - 1 + length - 1) // length)

    pair_blocks = [keyvals[0]]
    label_blocks = [documents[0]]
    place_blocks = [position * length + offsets]
    label_slab = jnp.broadcast_to(
        documents[0].astype(jnp.bfloat16)[:, None, None], (length, 1, pair_width)
    )
    packed = jnp.concatenate([keyvals[0], label_slab], axis=1)
    for hop in range(1, reach_hops + 1):
        arrived = shifted(packed, "ctx", hop)
        pair_blocks.append(arrived[:, :2])
        label_blocks.append(arrived[:, 2, 0].astype(jnp.int32))
        place_blocks.append((position - hop) * length + offsets)
    pairs = jnp.concatenate(pair_blocks, axis=0)
    pairs, anchor = lax.optimization_barrier((pairs, anchor))
    key_labels = jnp.concatenate(label_blocks, axis=0)
    key_place = jnp.concatenate(place_blocks, axis=0)
    key_count = pairs.shape[0]

    query_place = position * length + offsets
    query_labels = documents[0]
    query_block = queries[0].reshape(length, pair_heads, query_group_size, HEAD_DIM)
    key_block = pairs[:, 0].reshape(key_count, pair_heads, HEAD_DIM)
    value_block = pairs[:, 1].reshape(key_count, pair_heads, HEAD_DIM)

    scores = jnp.einsum(
        "qhgd,khd->hgqk", query_block, key_block, preferred_element_type=jnp.float32
    )
    scores = scores * (1.0 / math.sqrt(HEAD_DIM))
    allowed = (
        (query_labels[:, None] == key_labels[None, :])
        & (key_place[None, :] <= query_place[:, None])
        & (key_place[None, :] >= 0)
    )
    scores = jnp.where(allowed, scores, FLOOR_SCORE)
    peak = jnp.max(scores, axis=-1, keepdims=True)
    expo = jnp.where(allowed, jnp.exp(scores - peak), 0.0)
    total = jnp.sum(expo, axis=-1)
    summed = jnp.einsum(
        "hgqk,khd->qhgd",
        expo.astype(jnp.bfloat16),
        value_block,
        preferred_element_type=jnp.float32,
    )
    head_values = summed / jnp.transpose(total, (2, 0, 1))[..., None]
    head_values = head_values.reshape(length, pair_heads * query_group_size * HEAD_DIM)
    return head_values.astype(jnp.bfloat16), anchor


def swapped(block, axis):
    return lax.ppermute(block, axis, [(0, 1), (1, 0)])


def sent(block, route):
    return lax.ppermute(block, ("dp", "tensor"), route)


def needed_heads(head_values):
    group = lax.axis_size("tensor")
    me = lax.axis_index("tensor")
    side = lax.axis_index("dp")
    foreign = swapped(head_values, "dp")
    mine = jnp.concatenate([head_values, foreign], axis=1)
    owners = [(s, 2 * s + k) for s in range(2) for k in range(2)]
    over_y = sent(mine, [(s * group + p, s * group + (p ^ 2)) for s, p in owners])
    beside = sent(mine, [(s * group + p, s * group + (p ^ 1)) for s, p in owners])
    relayed = sent(
        over_y, [(s * group + (p ^ 2), s * group + (p ^ 3)) for s, p in owners]
    )
    on_owner = me // 2 == side
    same_core = jnp.where(on_owner, mine, over_y)
    other_core = jnp.where(on_owner, beside, relayed)
    first_core = me % 2 == 0
    width = head_values.shape[1]
    lower = jnp.where(first_core, same_core, other_core)
    upper = jnp.where(first_core, other_core, same_core)
    own_full = jnp.concatenate([lower[:, :width], upper[:, :width]], axis=1)
    foreign_full = jnp.concatenate([lower[:, width:], upper[:, width:]], axis=1)
    return own_full, foreign_full


def first_hop(block, axis):
    count = lax.axis_size(axis)
    rising = lax.ppermute(block, axis, [(i, i + 1) for i in range(count - 1)])
    falling = lax.ppermute(block, axis, [(i, i - 1) for i in range(1, count)])
    return rising, falling


def line_rows(block, first, axis):
    count = lax.axis_size(axis)
    here = lax.axis_index(axis)
    rising, falling = first
    arrivals = [(block, 0), (rising, -1), (falling, 1)]
    for step in range(2, count):
        rising = lax.ppermute(rising, axis, [(i, i + 1) for i in range(step - 1, count - 1)])
        falling = lax.ppermute(falling, axis, [(i, i - 1) for i in range(1, count - step + 1)])
        arrivals.append((rising, -step))
        arrivals.append((falling, step))
    ordered = []
    for place in range(count):
        chosen = jnp.zeros_like(block)
        for arrived, offset in arrivals:
            chosen = jnp.where(here + offset == place, arrived, chosen)
        ordered.append(chosen)
    return jnp.concatenate(ordered, axis=0)


def split_projection(head_values, side_rows):
    own_full, foreign_full = needed_heads(head_values)
    partner = jnp.dot(foreign_full, side_rows, preferred_element_type=jnp.float32)
    outgoing = partner.astype(jnp.bfloat16)
    returned = swapped(outgoing, "dp")
    outgoing, own_full, side_rows = lax.optimization_barrier((outgoing, own_full, side_rows))
    local = jnp.dot(own_full, side_rows, preferred_element_type=jnp.float32)
    local = lax.optimization_barrier(local)
    return local + returned.astype(jnp.float32)


def shards(queries, keyvals, documents, output_weight):
    block_rows = output_weight.shape[0]
    width = queries.shape[2]
    side_width = block_rows * lax.axis_size("ctx")
    fits = lax.axis_size("tensor") == 4
    if lax.axis_size("dp") == 2 and side_width == 2 * width and fits:
        first = first_hop(output_weight, "ctx")
        head_values, first = attention(queries, keyvals, documents, first)
        side_rows = line_rows(output_weight, first, "ctx")
        result = split_projection(head_values, side_rows)
        return result.astype(jnp.bfloat16)[None]
    all_rows = lax.all_gather(output_weight, ("dp", "ctx"), axis=0, tiled=True)
    head_values, _ = attention(queries, keyvals, documents, ())
    group = lax.axis_size("tensor")
    me = lax.axis_index("tensor")
    result = None
    for distance in range(group):
        held = head_values if distance == 0 else rotated(head_values, "tensor", distance)
        owner = (me - distance) % group
        rows = lax.dynamic_slice_in_dim(all_rows, owner * width, width, 0)
        part = jnp.dot(held, rows, preferred_element_type=jnp.float32)
        result = part if result is None else result + part
    return result.astype(jnp.bfloat16)[None]


def solution(mesh):
    placed = (
        P("dp", "ctx", "tensor"),
        P("dp", "ctx", None, "tensor"),
        P("dp", "ctx"),
        P(("dp", "ctx"), "tensor"),
    )
    return jax.shard_map(
        shards, mesh=mesh, in_specs=placed, out_specs=P("dp", "ctx", "tensor"), check_vma=False
    )
```

```python
import math

import jax
import jax.numpy as jnp
from jax import lax
from jax.sharding import PartitionSpec as P

HEAD_DIM = 128


FLOOR_SCORE = -1e30


def shifted(block, axis, distance):
    devices = range(lax.axis_size(axis))
    route = [(i - distance, i) for i in devices if i - distance in devices]
    return lax.ppermute(block, axis, route)


def rotated(block, axis, distance):
    count = lax.axis_size(axis)
    route = [(i, (i + distance) % count) for i in range(count)]
    return lax.ppermute(block, axis, route)


def attention(queries, keyvals, documents):
    length = queries.shape[1]
    pair_width = keyvals.shape[3]
    pair_heads = pair_width // HEAD_DIM
    query_group_size = queries.shape[2] // pair_width
    cycle_size = lax.axis_size("ctx")
    position = lax.axis_index("ctx")
    offsets = jnp.arange(length, dtype=jnp.int32)
    reach_hops = min(cycle_size - 1, (cycle_size * length // 2 - 1 + length - 1) // length)

    pair_blocks = [keyvals[0]]
    label_blocks = [documents[0]]
    place_blocks = [position * length + offsets]
    label_slab = jnp.broadcast_to(
        documents[0].astype(jnp.bfloat16)[:, None, None], (length, 1, pair_width)
    )
    packed = jnp.concatenate([keyvals[0], label_slab], axis=1)
    for hop in range(1, reach_hops + 1):
        arrived = shifted(packed, "ctx", hop)
        pair_blocks.append(arrived[:, :2])
        label_blocks.append(arrived[:, 2, 0].astype(jnp.int32))
        place_blocks.append((position - hop) * length + offsets)
    pairs = jnp.concatenate(pair_blocks, axis=0)
    key_labels = jnp.concatenate(label_blocks, axis=0)
    key_place = jnp.concatenate(place_blocks, axis=0)
    key_count = pairs.shape[0]

    query_place = position * length + offsets
    query_labels = documents[0]
    query_block = queries[0].reshape(length, pair_heads, query_group_size, HEAD_DIM)
    key_block = pairs[:, 0].reshape(key_count, pair_heads, HEAD_DIM)
    value_block = pairs[:, 1].reshape(key_count, pair_heads, HEAD_DIM)

    scores = jnp.einsum(
        "qhgd,khd->hgqk", query_block, key_block, preferred_element_type=jnp.float32
    )
    scores = scores * (1.0 / math.sqrt(HEAD_DIM))
    allowed = (
        (query_labels[:, None] == key_labels[None, :])
        & (key_place[None, :] <= query_place[:, None])
        & (key_place[None, :] >= 0)
    )
    scores = jnp.where(allowed, scores, FLOOR_SCORE)
    peak = jnp.max(scores, axis=-1, keepdims=True)
    expo = jnp.where(allowed, jnp.exp(scores - peak), 0.0)
    total = jnp.sum(expo, axis=-1)
    summed = jnp.einsum(
        "hgqk,khd->qhgd",
        expo.astype(jnp.bfloat16),
        value_block,
        preferred_element_type=jnp.float32,
    )
    head_values = summed / jnp.transpose(total, (2, 0, 1))[..., None]
    return head_values.reshape(length, pair_heads * query_group_size * HEAD_DIM).astype(
        jnp.bfloat16
    )


def swapped(block, axis):
    return lax.ppermute(block, axis, [(0, 1), (1, 0)])


def sent(block, route):
    return lax.ppermute(block, ("dp", "tensor"), route)


def needed_heads(head_values):
    group = lax.axis_size("tensor")
    me = lax.axis_index("tensor")
    side = lax.axis_index("dp")
    foreign = swapped(head_values, "dp")
    mine = jnp.concatenate([head_values, foreign], axis=1)
    owners = [(s, 2 * s + k) for s in range(2) for k in range(2)]
    over_y = sent(mine, [(s * group + p, s * group + (p ^ 2)) for s, p in owners])
    beside = sent(mine, [(s * group + p, s * group + (p ^ 1)) for s, p in owners])
    relayed = sent(
        over_y, [(s * group + (p ^ 2), s * group + (p ^ 3)) for s, p in owners]
    )
    on_owner = me // 2 == side
    same_core = jnp.where(on_owner, mine, over_y)
    other_core = jnp.where(on_owner, beside, relayed)
    first_core = me % 2 == 0
    width = head_values.shape[1]
    lower = jnp.where(first_core, same_core, other_core)
    upper = jnp.where(first_core, other_core, same_core)
    own_full = jnp.concatenate([lower[:, :width], upper[:, :width]], axis=1)
    foreign_full = jnp.concatenate([lower[:, width:], upper[:, width:]], axis=1)
    return own_full, foreign_full


def first_hop(block, axis):
    count = lax.axis_size(axis)
    far = count - 1
    rising = lax.ppermute(block, axis, [(i, i + 1) for i in range(count - 1)])
    falling = lax.ppermute(block, axis, [(i, i - 1) for i in range(1, count)])
    far_rising = lax.ppermute(block, axis, [(i, i + far) for i in range(count - far)])
    far_falling = lax.ppermute(block, axis, [(i + far, i) for i in range(count - far)])
    return rising, falling, far_rising, far_falling


def line_rows(block, first, axis):
    count = lax.axis_size(axis)
    here = lax.axis_index(axis)
    rising, falling, far_rising, far_falling = first
    far = count - 1
    arrivals = [(block, 0), (rising, -1), (falling, 1)]
    if far > 1:
        arrivals += [(far_rising, -far), (far_falling, far)]
    for step in range(2, far):
        rising = lax.ppermute(rising, axis, [(i, i + 1) for i in range(step - 1, count - 1)])
        falling = lax.ppermute(falling, axis, [(i, i - 1) for i in range(1, count - step + 1)])
        arrivals.append((rising, -step))
        arrivals.append((falling, step))
    ordered = []
    for place in range(count):
        chosen = jnp.zeros_like(block)
        for arrived, offset in arrivals:
            chosen = jnp.where(here + offset == place, arrived, chosen)
        ordered.append(chosen)
    return jnp.concatenate(ordered, axis=0)


def split_projection(head_values, side_rows):
    own_full, foreign_full = needed_heads(head_values)
    partner = jnp.dot(foreign_full, side_rows, preferred_element_type=jnp.float32)
    outgoing = partner.astype(jnp.bfloat16)
    returned = swapped(outgoing, "dp")
    outgoing, own_full, side_rows = lax.optimization_barrier((outgoing, own_full, side_rows))
    local = jnp.dot(own_full, side_rows, preferred_element_type=jnp.float32)
    local = lax.optimization_barrier(local)
    return local + returned.astype(jnp.float32)


def shards(queries, keyvals, documents, output_weight):
    block_rows = output_weight.shape[0]
    width = queries.shape[2]
    side_width = block_rows * lax.axis_size("ctx")
    fits = lax.axis_size("tensor") == 4
    if lax.axis_size("dp") == 2 and side_width == 2 * width and fits:
        first = first_hop(output_weight, "ctx")
        head_values = attention(queries, keyvals, documents)
        first, head_values = lax.optimization_barrier((first, head_values))
        side_rows = line_rows(output_weight, first, "ctx")
        result = split_projection(head_values, side_rows)
        return result.astype(jnp.bfloat16)[None]
    all_rows = lax.all_gather(output_weight, ("dp", "ctx"), axis=0, tiled=True)
    head_values = attention(queries, keyvals, documents)
    group = lax.axis_size("tensor")
    me = lax.axis_index("tensor")
    result = None
    for distance in range(group):
        held = head_values if distance == 0 else rotated(head_values, "tensor", distance)
        owner = (me - distance) % group
        rows = lax.dynamic_slice_in_dim(all_rows, owner * width, width, 0)
        part = jnp.dot(held, rows, preferred_element_type=jnp.float32)
        result = part if result is None else result + part
    return result.astype(jnp.bfloat16)[None]


def solution(mesh):
    placed = (
        P("dp", "ctx", "tensor"),
        P("dp", "ctx", None, "tensor"),
        P("dp", "ctx"),
        P(("dp", "ctx"), "tensor"),
    )
    return jax.shard_map(
        shards, mesh=mesh, in_specs=placed, out_specs=P("dp", "ctx", "tensor"), check_vma=False
    )
```

```python
import math

import jax
import jax.numpy as jnp
from jax import lax
from jax.sharding import PartitionSpec as P

HEAD_DIM = 128


FLOOR_SCORE = -1e30


def shifted(block, axis, distance):
    devices = range(lax.axis_size(axis))
    route = [(i - distance, i) for i in devices if i - distance in devices]
    return lax.ppermute(block, axis, route)


def rotated(block, axis, distance):
    count = lax.axis_size(axis)
    route = [(i, (i + distance) % count) for i in range(count)]
    return lax.ppermute(block, axis, route)


def packed_keys(keyvals, documents):
    length = keyvals.shape[1]
    label_slab = jnp.broadcast_to(
        documents[0].astype(jnp.bfloat16)[:, None, None], (length, 1, keyvals.shape[3])
    )
    return jnp.concatenate([keyvals[0], label_slab], axis=1)


def reach_of(length):
    cycle_size = lax.axis_size("ctx")
    return min(cycle_size - 1, (cycle_size * length // 2 - 1 + length - 1) // length)


def attention(queries, keyvals, documents, arrived):
    length = queries.shape[1]
    pair_width = keyvals.shape[3]
    pair_heads = pair_width // HEAD_DIM
    query_group_size = queries.shape[2] // pair_width
    position = lax.axis_index("ctx")
    offsets = jnp.arange(length, dtype=jnp.int32)

    pair_blocks = [keyvals[0]]
    label_blocks = [documents[0]]
    place_blocks = [position * length + offsets]
    for hop, block in enumerate(arrived, start=1):
        pair_blocks.append(block[:, :2])
        label_blocks.append(block[:, 2, 0].astype(jnp.int32))
        place_blocks.append((position - hop) * length + offsets)
    pairs = jnp.concatenate(pair_blocks, axis=0)
    key_labels = jnp.concatenate(label_blocks, axis=0)
    key_place = jnp.concatenate(place_blocks, axis=0)
    key_count = pairs.shape[0]

    query_place = position * length + offsets
    query_labels = documents[0]
    query_block = queries[0].reshape(length, pair_heads, query_group_size, HEAD_DIM)
    key_block = pairs[:, 0].reshape(key_count, pair_heads, HEAD_DIM)
    value_block = pairs[:, 1].reshape(key_count, pair_heads, HEAD_DIM)

    scores = jnp.einsum(
        "qhgd,khd->hgqk", query_block, key_block, preferred_element_type=jnp.float32
    )
    scores = scores * (1.0 / math.sqrt(HEAD_DIM))
    allowed = (
        (query_labels[:, None] == key_labels[None, :])
        & (key_place[None, :] <= query_place[:, None])
        & (key_place[None, :] >= 0)
    )
    scores = jnp.where(allowed, scores, FLOOR_SCORE)
    peak = jnp.max(scores, axis=-1, keepdims=True)
    expo = jnp.where(allowed, jnp.exp(scores - peak), 0.0)
    total = jnp.sum(expo, axis=-1)
    summed = jnp.einsum(
        "hgqk,khd->qhgd",
        expo.astype(jnp.bfloat16),
        value_block,
        preferred_element_type=jnp.float32,
    )
    head_values = summed / jnp.transpose(total, (2, 0, 1))[..., None]
    return head_values.reshape(length, pair_heads * query_group_size * HEAD_DIM).astype(
        jnp.bfloat16
    )


def swapped(block, axis):
    return lax.ppermute(block, axis, [(0, 1), (1, 0)])


def sent(block, route):
    return lax.ppermute(block, ("dp", "tensor"), route)


def needed_heads(head_values):
    group = lax.axis_size("tensor")
    me = lax.axis_index("tensor")
    side = lax.axis_index("dp")
    foreign = swapped(head_values, "dp")
    mine = jnp.concatenate([head_values, foreign], axis=1)
    owners = [(s, 2 * s + k) for s in range(2) for k in range(2)]
    over_y = sent(mine, [(s * group + p, s * group + (p ^ 2)) for s, p in owners])
    beside = sent(mine, [(s * group + p, s * group + (p ^ 1)) for s, p in owners])
    relayed = sent(
        over_y, [(s * group + (p ^ 2), s * group + (p ^ 3)) for s, p in owners]
    )
    on_owner = me // 2 == side
    same_core = jnp.where(on_owner, mine, over_y)
    other_core = jnp.where(on_owner, beside, relayed)
    first_core = me % 2 == 0
    width = head_values.shape[1]
    lower = jnp.where(first_core, same_core, other_core)
    upper = jnp.where(first_core, other_core, same_core)
    own_full = jnp.concatenate([lower[:, :width], upper[:, :width]], axis=1)
    foreign_full = jnp.concatenate([lower[:, width:], upper[:, width:]], axis=1)
    return own_full, foreign_full


def first_hop(block, axis):
    count = lax.axis_size(axis)
    rising = lax.ppermute(block, axis, [(i, i + 1) for i in range(count - 1)])
    falling = lax.ppermute(block, axis, [(i, i - 1) for i in range(1, count)])
    return rising, falling


def line_rows(block, first, axis):
    count = lax.axis_size(axis)
    here = lax.axis_index(axis)
    rising, falling = first
    arrivals = [(block, 0), (rising, -1), (falling, 1)]
    for step in range(2, count):
        rising = lax.ppermute(rising, axis, [(i, i + 1) for i in range(step - 1, count - 1)])
        falling = lax.ppermute(falling, axis, [(i, i - 1) for i in range(1, count - step + 1)])
        arrivals.append((rising, -step))
        arrivals.append((falling, step))
    ordered = []
    for place in range(count):
        chosen = jnp.zeros_like(block)
        for arrived, offset in arrivals:
            chosen = jnp.where(here + offset == place, arrived, chosen)
        ordered.append(chosen)
    return jnp.concatenate(ordered, axis=0)


def split_projection(head_values, side_rows):
    own_full, foreign_full = needed_heads(head_values)
    partner = jnp.dot(foreign_full, side_rows, preferred_element_type=jnp.float32)
    outgoing = partner.astype(jnp.bfloat16)
    returned = swapped(outgoing, "dp")
    outgoing, own_full, side_rows = lax.optimization_barrier((outgoing, own_full, side_rows))
    local = jnp.dot(own_full, side_rows, preferred_element_type=jnp.float32)
    local = lax.optimization_barrier(local)
    return local + returned.astype(jnp.float32)


def shards(queries, keyvals, documents, output_weight):
    block_rows = output_weight.shape[0]
    width = queries.shape[2]
    side_width = block_rows * lax.axis_size("ctx")
    fits = lax.axis_size("tensor") == 4
    fits = fits and reach_of(queries.shape[1]) >= 1
    if lax.axis_size("dp") == 2 and side_width == 2 * width and fits:
        count = lax.axis_size("ctx")
        columns = output_weight.shape[1]
        packed = packed_keys(keyvals, documents)
        joined = jnp.concatenate([output_weight, packed.reshape(packed.shape[0], -1)], axis=1)
        joined = lax.ppermute(joined, "ctx", [(i, i + 1) for i in range(count - 1)])
        rising = joined[:, :columns]
        nearest = joined[:, columns:].reshape(packed.shape)
        falling = lax.ppermute(output_weight, "ctx", [(i, i - 1) for i in range(1, count)])
        farther = [shifted(packed, "ctx", hop) for hop in range(2, reach_of(queries.shape[1]) + 1)]
        falling, farther = lax.optimization_barrier((falling, farther))
        head_values = attention(queries, keyvals, documents, [nearest] + farther)
        side_rows = line_rows(output_weight, (rising, falling), "ctx")
        result = split_projection(head_values, side_rows)
        return result.astype(jnp.bfloat16)[None]
    all_rows = lax.all_gather(output_weight, ("dp", "ctx"), axis=0, tiled=True)
    packed = packed_keys(keyvals, documents)
    arrived = [shifted(packed, "ctx", hop) for hop in range(1, reach_of(queries.shape[1]) + 1)]
    head_values = attention(queries, keyvals, documents, arrived)
    group = lax.axis_size("tensor")
    me = lax.axis_index("tensor")
    result = None
    for distance in range(group):
        held = head_values if distance == 0 else rotated(head_values, "tensor", distance)
        owner = (me - distance) % group
        rows = lax.dynamic_slice_in_dim(all_rows, owner * width, width, 0)
        part = jnp.dot(held, rows, preferred_element_type=jnp.float32)
        result = part if result is None else result + part
    return result.astype(jnp.bfloat16)[None]


def solution(mesh):
    placed = (
        P("dp", "ctx", "tensor"),
        P("dp", "ctx", None, "tensor"),
        P("dp", "ctx"),
        P(("dp", "ctx"), "tensor"),
    )
    return jax.shard_map(
        shards, mesh=mesh, in_specs=placed, out_specs=P("dp", "ctx", "tensor"), check_vma=False
    )
```

```python
import math

import jax
import jax.numpy as jnp
from jax import lax
from jax.sharding import PartitionSpec as P

HEAD_DIM = 128


FLOOR_SCORE = -1e30


def shifted(block, axis, distance):
    devices = range(lax.axis_size(axis))
    route = [(i - distance, i) for i in devices if i - distance in devices]
    return lax.ppermute(block, axis, route)


def rotated(block, axis, distance):
    count = lax.axis_size(axis)
    route = [(i, (i + distance) % count) for i in range(count)]
    return lax.ppermute(block, axis, route)


def attention(queries, keyvals, documents):
    length = queries.shape[1]
    pair_width = keyvals.shape[3]
    pair_heads = pair_width // HEAD_DIM
    query_group_size = queries.shape[2] // pair_width
    cycle_size = lax.axis_size("ctx")
    position = lax.axis_index("ctx")
    offsets = jnp.arange(length, dtype=jnp.int32)
    reach_hops = min(cycle_size - 1, (cycle_size * length // 2 - 1 + length - 1) // length)

    pair_blocks = [keyvals[0]]
    label_blocks = [documents[0]]
    place_blocks = [position * length + offsets]
    label_slab = jnp.broadcast_to(
        documents[0].astype(jnp.bfloat16)[:, None, None], (length, 1, pair_width)
    )
    packed = jnp.concatenate([keyvals[0], label_slab], axis=1)
    for hop in range(1, reach_hops + 1):
        arrived = shifted(packed, "ctx", hop)
        pair_blocks.append(arrived[:, :2])
        label_blocks.append(arrived[:, 2, 0].astype(jnp.int32))
        place_blocks.append((position - hop) * length + offsets)
    pairs = jnp.concatenate(pair_blocks, axis=0)
    key_labels = jnp.concatenate(label_blocks, axis=0)
    key_place = jnp.concatenate(place_blocks, axis=0)
    key_count = pairs.shape[0]

    query_place = position * length + offsets
    query_labels = documents[0]
    query_block = queries[0].reshape(length, pair_heads, query_group_size, HEAD_DIM)
    key_block = pairs[:, 0].reshape(key_count, pair_heads, HEAD_DIM)
    value_block = pairs[:, 1].reshape(key_count, pair_heads, HEAD_DIM)

    scores = jnp.einsum(
        "qhgd,khd->hgqk", query_block, key_block, preferred_element_type=jnp.float32
    )
    scores = scores * (1.0 / math.sqrt(HEAD_DIM))
    allowed = (
        (query_labels[:, None] == key_labels[None, :])
        & (key_place[None, :] <= query_place[:, None])
        & (key_place[None, :] >= 0)
    )
    scores = jnp.where(allowed, scores, FLOOR_SCORE)
    peak = jnp.max(scores, axis=-1, keepdims=True)
    expo = jnp.where(allowed, jnp.exp(scores - peak), 0.0)
    total = jnp.sum(expo, axis=-1)
    summed = jnp.einsum(
        "hgqk,khd->qhgd",
        expo.astype(jnp.bfloat16),
        value_block,
        preferred_element_type=jnp.float32,
    )
    head_values = summed / jnp.transpose(total, (2, 0, 1))[..., None]
    return head_values.reshape(length, pair_heads * query_group_size * HEAD_DIM).astype(
        jnp.bfloat16
    )


def swapped(block, axis):
    return lax.ppermute(block, axis, [(0, 1), (1, 0)])


def sent(block, route):
    return lax.ppermute(block, ("dp", "tensor"), route)


def needed_heads(head_values):
    group = lax.axis_size("tensor")
    me = lax.axis_index("tensor")
    side = lax.axis_index("dp")
    foreign = swapped(head_values, "dp")
    mine = jnp.concatenate([head_values, foreign], axis=1)
    owners = [(s, 2 * s + k) for s in range(2) for k in range(2)]
    over_y = sent(mine, [(s * group + p, s * group + (p ^ 2)) for s, p in owners])
    beside = sent(mine, [(s * group + p, s * group + (p ^ 1)) for s, p in owners])
    relayed = sent(
        over_y, [(s * group + (p ^ 2), s * group + (p ^ 3)) for s, p in owners]
    )
    on_owner = me // 2 == side
    same_core = jnp.where(on_owner, mine, over_y)
    other_core = jnp.where(on_owner, beside, relayed)
    first_core = me % 2 == 0
    width = head_values.shape[1]
    lower = jnp.where(first_core, same_core, other_core)
    upper = jnp.where(first_core, other_core, same_core)
    own_full = jnp.concatenate([lower[:, :width], upper[:, :width]], axis=1)
    foreign_full = jnp.concatenate([lower[:, width:], upper[:, width:]], axis=1)
    return own_full, foreign_full


def first_hop(block, axis):
    count = lax.axis_size(axis)
    rising = lax.ppermute(block, axis, [(i, i + 1) for i in range(count - 1)])
    falling = lax.ppermute(block, axis, [(i, i - 1) for i in range(1, count)])
    return rising, falling


def line_rows(block, first, axis, late_block):
    count = lax.axis_size(axis)
    here = lax.axis_index(axis)
    rising, falling = first
    arrivals = [(block, 0), (rising, -1), (falling, 1)]
    far = count - 1
    if far > 1:
        far_rising = lax.ppermute(late_block, axis, [(i, i + far) for i in range(count - far)])
        far_falling = lax.ppermute(late_block, axis, [(i + far, i) for i in range(count - far)])
        arrivals += [(far_rising, -far), (far_falling, far)]
    for step in range(2, far):
        rising = lax.ppermute(rising, axis, [(i, i + 1) for i in range(step - 1, count - 1)])
        falling = lax.ppermute(falling, axis, [(i, i - 1) for i in range(1, count - step + 1)])
        arrivals.append((rising, -step))
        arrivals.append((falling, step))
    ordered = []
    for place in range(count):
        chosen = jnp.zeros_like(block)
        for arrived, offset in arrivals:
            chosen = jnp.where(here + offset == place, arrived, chosen)
        ordered.append(chosen)
    return jnp.concatenate(ordered, axis=0)


def split_projection(head_values, side_rows):
    own_full, foreign_full = needed_heads(head_values)
    partner = jnp.dot(foreign_full, side_rows, preferred_element_type=jnp.float32)
    outgoing = partner.astype(jnp.bfloat16)
    returned = swapped(outgoing, "dp")
    outgoing, own_full, side_rows = lax.optimization_barrier((outgoing, own_full, side_rows))
    local = jnp.dot(own_full, side_rows, preferred_element_type=jnp.float32)
    local = lax.optimization_barrier(local)
    return local + returned.astype(jnp.float32)


def shards(queries, keyvals, documents, output_weight):
    block_rows = output_weight.shape[0]
    width = queries.shape[2]
    side_width = block_rows * lax.axis_size("ctx")
    fits = lax.axis_size("tensor") == 4
    if lax.axis_size("dp") == 2 and side_width == 2 * width and fits:
        first = first_hop(output_weight, "ctx")
        head_values = attention(queries, keyvals, documents)
        first, head_values, late_block = lax.optimization_barrier((first, head_values, output_weight))
        side_rows = line_rows(output_weight, first, "ctx", late_block)
        result = split_projection(head_values, side_rows)
        return result.astype(jnp.bfloat16)[None]
    all_rows = lax.all_gather(output_weight, ("dp", "ctx"), axis=0, tiled=True)
    head_values = attention(queries, keyvals, documents)
    group = lax.axis_size("tensor")
    me = lax.axis_index("tensor")
    result = None
    for distance in range(group):
        held = head_values if distance == 0 else rotated(head_values, "tensor", distance)
        owner = (me - distance) % group
        rows = lax.dynamic_slice_in_dim(all_rows, owner * width, width, 0)
        part = jnp.dot(held, rows, preferred_element_type=jnp.float32)
        result = part if result is None else result + part
    return result.astype(jnp.bfloat16)[None]


def solution(mesh):
    placed = (
        P("dp", "ctx", "tensor"),
        P("dp", "ctx", None, "tensor"),
        P("dp", "ctx"),
        P(("dp", "ctx"), "tensor"),
    )
    return jax.shard_map(
        shards, mesh=mesh, in_specs=placed, out_specs=P("dp", "ctx", "tensor"), check_vma=False
    )
```

```python
import math

import jax
import jax.numpy as jnp
from jax import lax
from jax.sharding import PartitionSpec as P

HEAD_DIM = 128


FLOOR_SCORE = -1e30


def shifted(block, axis, distance):
    devices = range(lax.axis_size(axis))
    route = [(i - distance, i) for i in devices if i - distance in devices]
    return lax.ppermute(block, axis, route)


def rotated(block, axis, distance):
    count = lax.axis_size(axis)
    route = [(i, (i + distance) % count) for i in range(count)]
    return lax.ppermute(block, axis, route)


def attention(queries, keyvals, documents):
    length = queries.shape[1]
    pair_width = keyvals.shape[3]
    pair_heads = pair_width // HEAD_DIM
    query_group_size = queries.shape[2] // pair_width
    cycle_size = lax.axis_size("ctx")
    position = lax.axis_index("ctx")
    offsets = jnp.arange(length, dtype=jnp.int32)
    reach_hops = min(cycle_size - 1, (cycle_size * length // 2 - 1 + length - 1) // length)

    pair_blocks = [keyvals[0]]
    label_blocks = [documents[0]]
    place_blocks = [position * length + offsets]
    label_slab = jnp.broadcast_to(
        documents[0].astype(jnp.bfloat16)[:, None, None], (length, 1, pair_width)
    )
    packed = jnp.concatenate([keyvals[0], label_slab], axis=1)
    for hop in range(1, reach_hops + 1):
        arrived = shifted(packed, "ctx", hop)
        pair_blocks.append(arrived[:, :2])
        label_blocks.append(arrived[:, 2, 0].astype(jnp.int32))
        place_blocks.append((position - hop) * length + offsets)
    pairs = jnp.concatenate(pair_blocks, axis=0)
    key_labels = jnp.concatenate(label_blocks, axis=0)
    key_place = jnp.concatenate(place_blocks, axis=0)
    key_count = pairs.shape[0]

    query_place = position * length + offsets
    query_labels = documents[0]
    query_block = queries[0].reshape(length, pair_heads, query_group_size, HEAD_DIM)
    key_block = pairs[:, 0].reshape(key_count, pair_heads, HEAD_DIM)
    value_block = pairs[:, 1].reshape(key_count, pair_heads, HEAD_DIM)

    scores = jnp.einsum(
        "qhgd,khd->hgqk", query_block, key_block, preferred_element_type=jnp.float32
    )
    scores = scores * (1.0 / math.sqrt(HEAD_DIM))
    allowed = (
        (query_labels[:, None] == key_labels[None, :])
        & (key_place[None, :] <= query_place[:, None])
        & (key_place[None, :] >= 0)
    )
    scores = jnp.where(allowed, scores, FLOOR_SCORE)
    peak = jnp.max(scores, axis=-1, keepdims=True)
    expo = jnp.where(allowed, jnp.exp(scores - peak), 0.0)
    total = jnp.sum(expo, axis=-1)
    summed = jnp.einsum(
        "hgqk,khd->qhgd",
        expo.astype(jnp.bfloat16),
        value_block,
        preferred_element_type=jnp.float32,
    )
    head_values = summed / jnp.transpose(total, (2, 0, 1))[..., None]
    return head_values.reshape(length, pair_heads * query_group_size * HEAD_DIM).astype(
        jnp.bfloat16
    )


def swapped(block, axis):
    return lax.ppermute(block, axis, [(0, 1), (1, 0)])


def sent(block, route):
    return lax.ppermute(block, ("dp", "tensor"), route)


def needed_heads(head_values):
    group = lax.axis_size("tensor")
    me = lax.axis_index("tensor")
    side = lax.axis_index("dp")
    width = head_values.shape[1]
    owners = [(s, 2 * s + k) for s in range(2) for k in range(2)]
    over_y = [(s * group + p, s * group + (p ^ 2)) for s, p in owners]
    foreign = swapped(head_values, "dp")
    own_over = sent(head_values, over_y)
    foreign_over = sent(foreign, over_y)
    on_owner = me // 2 == side
    own_same = jnp.where(on_owner, head_values, own_over)
    foreign_same = jnp.where(on_owner, foreign, foreign_over)
    both_same = jnp.concatenate([own_same, foreign_same], axis=1)
    both_other = lax.ppermute(both_same, "tensor", [(t, t ^ 1) for t in range(group)])
    first_core = me % 2 == 0
    lower = jnp.where(first_core, both_same, both_other)
    upper = jnp.where(first_core, both_other, both_same)
    own_full = jnp.concatenate([lower[:, :width], upper[:, :width]], axis=1)
    foreign_full = jnp.concatenate([lower[:, width:], upper[:, width:]], axis=1)
    return own_full, foreign_full


def first_hop(block, axis):
    count = lax.axis_size(axis)
    rising = lax.ppermute(block, axis, [(i, i + 1) for i in range(count - 1)])
    falling = lax.ppermute(block, axis, [(i, i - 1) for i in range(1, count)])
    return rising, falling


def line_rows(block, first, axis, late_block):
    count = lax.axis_size(axis)
    here = lax.axis_index(axis)
    rising, falling = first
    arrivals = [(block, 0), (rising, -1), (falling, 1)]
    far = count - 1
    if far > 1:
        far_rising = lax.ppermute(late_block, axis, [(i, i + far) for i in range(count - far)])
        far_falling = lax.ppermute(late_block, axis, [(i + far, i) for i in range(count - far)])
        arrivals += [(far_rising, -far), (far_falling, far)]
    for step in range(2, far):
        rising = lax.ppermute(rising, axis, [(i, i + 1) for i in range(step - 1, count - 1)])
        falling = lax.ppermute(falling, axis, [(i, i - 1) for i in range(1, count - step + 1)])
        arrivals.append((rising, -step))
        arrivals.append((falling, step))
    ordered = []
    for place in range(count):
        chosen = jnp.zeros_like(block)
        for arrived, offset in arrivals:
            chosen = jnp.where(here + offset == place, arrived, chosen)
        ordered.append(chosen)
    return jnp.concatenate(ordered, axis=0)


def split_projection(head_values, side_rows):
    own_full, foreign_full = needed_heads(head_values)
    partner = jnp.dot(foreign_full, side_rows, preferred_element_type=jnp.float32)
    outgoing = partner.astype(jnp.bfloat16)
    returned = swapped(outgoing, "dp")
    outgoing, own_full, side_rows = lax.optimization_barrier((outgoing, own_full, side_rows))
    local = jnp.dot(own_full, side_rows, preferred_element_type=jnp.float32)
    local = lax.optimization_barrier(local)
    return local + returned.astype(jnp.float32)


def shards(queries, keyvals, documents, output_weight):
    block_rows = output_weight.shape[0]
    width = queries.shape[2]
    side_width = block_rows * lax.axis_size("ctx")
    fits = lax.axis_size("tensor") == 4
    if lax.axis_size("dp") == 2 and side_width == 2 * width and fits:
        first = first_hop(output_weight, "ctx")
        head_values = attention(queries, keyvals, documents)
        first, head_values, late_block = lax.optimization_barrier((first, head_values, output_weight))
        side_rows = line_rows(output_weight, first, "ctx", late_block)
        result = split_projection(head_values, side_rows)
        return result.astype(jnp.bfloat16)[None]
    all_rows = lax.all_gather(output_weight, ("dp", "ctx"), axis=0, tiled=True)
    head_values = attention(queries, keyvals, documents)
    group = lax.axis_size("tensor")
    me = lax.axis_index("tensor")
    result = None
    for distance in range(group):
        held = head_values if distance == 0 else rotated(head_values, "tensor", distance)
        owner = (me - distance) % group
        rows = lax.dynamic_slice_in_dim(all_rows, owner * width, width, 0)
        part = jnp.dot(held, rows, preferred_element_type=jnp.float32)
        result = part if result is None else result + part
    return result.astype(jnp.bfloat16)[None]


def solution(mesh):
    placed = (
        P("dp", "ctx", "tensor"),
        P("dp", "ctx", None, "tensor"),
        P("dp", "ctx"),
        P(("dp", "ctx"), "tensor"),
    )
    return jax.shard_map(
        shards, mesh=mesh, in_specs=placed, out_specs=P("dp", "ctx", "tensor"), check_vma=False
    )
```

```python
import math

import jax
import jax.numpy as jnp
from jax import lax
from jax.sharding import PartitionSpec as P

HEAD_DIM = 128


FLOOR_SCORE = -1e30


def shifted(block, axis, distance):
    devices = range(lax.axis_size(axis))
    route = [(i - distance, i) for i in devices if i - distance in devices]
    return lax.ppermute(block, axis, route)


def rotated(block, axis, distance):
    count = lax.axis_size(axis)
    route = [(i, (i + distance) % count) for i in range(count)]
    return lax.ppermute(block, axis, route)


def packed_keys(keyvals, documents):
    length = keyvals.shape[1]
    label_slab = jnp.broadcast_to(
        documents[0].astype(jnp.bfloat16)[:, None, None], (length, 1, keyvals.shape[3])
    )
    return jnp.concatenate([keyvals[0], label_slab], axis=1)


def reach_of(length):
    cycle_size = lax.axis_size("ctx")
    return min(cycle_size - 1, (cycle_size * length // 2 - 1 + length - 1) // length)


def attention(queries, keyvals, documents, arrived):
    length = queries.shape[1]
    pair_width = keyvals.shape[3]
    pair_heads = pair_width // HEAD_DIM
    query_group_size = queries.shape[2] // pair_width
    position = lax.axis_index("ctx")
    offsets = jnp.arange(length, dtype=jnp.int32)

    pair_blocks = [keyvals[0]]
    label_blocks = [documents[0]]
    place_blocks = [position * length + offsets]
    for hop, block in enumerate(arrived, start=1):
        pair_blocks.append(block[:, :2])
        label_blocks.append(block[:, 2, 0].astype(jnp.int32))
        place_blocks.append((position - hop) * length + offsets)
    pairs = jnp.concatenate(pair_blocks, axis=0)
    key_labels = jnp.concatenate(label_blocks, axis=0)
    key_place = jnp.concatenate(place_blocks, axis=0)
    key_count = pairs.shape[0]

    query_place = position * length + offsets
    query_labels = documents[0]
    query_block = queries[0].reshape(length, pair_heads, query_group_size, HEAD_DIM)
    key_block = pairs[:, 0].reshape(key_count, pair_heads, HEAD_DIM)
    value_block = pairs[:, 1].reshape(key_count, pair_heads, HEAD_DIM)

    scores = jnp.einsum(
        "qhgd,khd->hgqk", query_block, key_block, preferred_element_type=jnp.float32
    )
    scores = scores * (1.0 / math.sqrt(HEAD_DIM))
    allowed = (
        (query_labels[:, None] == key_labels[None, :])
        & (key_place[None, :] <= query_place[:, None])
        & (key_place[None, :] >= 0)
    )
    scores = jnp.where(allowed, scores, FLOOR_SCORE)
    peak = jnp.max(scores, axis=-1, keepdims=True)
    expo = jnp.where(allowed, jnp.exp(scores - peak), 0.0)
    total = jnp.sum(expo, axis=-1)
    summed = jnp.einsum(
        "hgqk,khd->qhgd",
        expo.astype(jnp.bfloat16),
        value_block,
        preferred_element_type=jnp.float32,
    )
    head_values = summed / jnp.transpose(total, (2, 0, 1))[..., None]
    return head_values.reshape(length, pair_heads * query_group_size * HEAD_DIM).astype(
        jnp.bfloat16
    )


def swapped(block, axis):
    return lax.ppermute(block, axis, [(0, 1), (1, 0)])


def sent(block, route):
    return lax.ppermute(block, ("dp", "tensor"), route)


def needed_heads(head_values):
    group = lax.axis_size("tensor")
    me = lax.axis_index("tensor")
    side = lax.axis_index("dp")
    foreign = swapped(head_values, "dp")
    mine = jnp.concatenate([head_values, foreign], axis=1)
    owners = [(s, 2 * s + k) for s in range(2) for k in range(2)]
    over_y = sent(mine, [(s * group + p, s * group + (p ^ 2)) for s, p in owners])
    beside = sent(mine, [(s * group + p, s * group + (p ^ 1)) for s, p in owners])
    relayed = sent(
        over_y, [(s * group + (p ^ 2), s * group + (p ^ 3)) for s, p in owners]
    )
    on_owner = me // 2 == side
    same_core = jnp.where(on_owner, mine, over_y)
    other_core = jnp.where(on_owner, beside, relayed)
    first_core = me % 2 == 0
    width = head_values.shape[1]
    lower = jnp.where(first_core, same_core, other_core)
    upper = jnp.where(first_core, other_core, same_core)
    own_full = jnp.concatenate([lower[:, :width], upper[:, :width]], axis=1)
    foreign_full = jnp.concatenate([lower[:, width:], upper[:, width:]], axis=1)
    return own_full, foreign_full


def line_rows(block, first, axis):
    count = lax.axis_size(axis)
    here = lax.axis_index(axis)
    rising, falling = first
    arrivals = [(block, 0), (rising, -1), (falling, 1)]
    for step in range(2, count):
        rising = lax.ppermute(rising, axis, [(i, i + 1) for i in range(step - 1, count - 1)])
        falling = lax.ppermute(falling, axis, [(i, i - 1) for i in range(1, count - step + 1)])
        arrivals.append((rising, -step))
        arrivals.append((falling, step))
    ordered = []
    for place in range(count):
        chosen = jnp.zeros_like(block)
        for arrived, offset in arrivals:
            chosen = jnp.where(here + offset == place, arrived, chosen)
        ordered.append(chosen)
    return jnp.concatenate(ordered, axis=0)


def split_projection(head_values, side_rows):
    own_full, foreign_full = needed_heads(head_values)
    partner = jnp.dot(foreign_full, side_rows, preferred_element_type=jnp.float32)
    outgoing = partner.astype(jnp.bfloat16)
    returned = swapped(outgoing, "dp")
    outgoing, own_full, side_rows = lax.optimization_barrier((outgoing, own_full, side_rows))
    local = jnp.dot(own_full, side_rows, preferred_element_type=jnp.float32)
    local = lax.optimization_barrier(local)
    return local + returned.astype(jnp.float32)


def shards(queries, keyvals, documents, output_weight):
    block_rows = output_weight.shape[0]
    width = queries.shape[2]
    side_width = block_rows * lax.axis_size("ctx")
    fits = lax.axis_size("tensor") == 4
    fits = fits and reach_of(queries.shape[1]) >= 1
    if lax.axis_size("dp") == 2 and side_width == 2 * width and fits:
        count = lax.axis_size("ctx")
        columns = output_weight.shape[1]
        packed = packed_keys(keyvals, documents)
        joined = jnp.concatenate([output_weight, packed.reshape(packed.shape[0], -1)], axis=1)
        joined = lax.ppermute(joined, "ctx", [(i, i + 1) for i in range(count - 1)])
        rising = joined[:, :columns]
        nearest = joined[:, columns:].reshape(packed.shape)
        falling = lax.ppermute(output_weight, "ctx", [(i, i - 1) for i in range(1, count)])
        farther = [shifted(packed, "ctx", hop) for hop in range(2, reach_of(queries.shape[1]) + 1)]
        head_values = attention(queries, keyvals, documents, [nearest] + farther)
        falling, head_values = lax.optimization_barrier((falling, head_values))
        side_rows = line_rows(output_weight, (rising, falling), "ctx")
        result = split_projection(head_values, side_rows)
        return result.astype(jnp.bfloat16)[None]
    all_rows = lax.all_gather(output_weight, ("dp", "ctx"), axis=0, tiled=True)
    packed = packed_keys(keyvals, documents)
    arrived = [shifted(packed, "ctx", hop) for hop in range(1, reach_of(queries.shape[1]) + 1)]
    head_values = attention(queries, keyvals, documents, arrived)
    group = lax.axis_size("tensor")
    me = lax.axis_index("tensor")
    result = None
    for distance in range(group):
        held = head_values if distance == 0 else rotated(head_values, "tensor", distance)
        owner = (me - distance) % group
        rows = lax.dynamic_slice_in_dim(all_rows, owner * width, width, 0)
        part = jnp.dot(held, rows, preferred_element_type=jnp.float32)
        result = part if result is None else result + part
    return result.astype(jnp.bfloat16)[None]


def solution(mesh):
    placed = (
        P("dp", "ctx", "tensor"),
        P("dp", "ctx", None, "tensor"),
        P("dp", "ctx"),
        P(("dp", "ctx"), "tensor"),
    )
    return jax.shard_map(
        shards, mesh=mesh, in_specs=placed, out_specs=P("dp", "ctx", "tensor"), check_vma=False
    )
```

```python
import math

import jax
import jax.numpy as jnp
from jax import lax
from jax.sharding import PartitionSpec as P

HEAD_DIM = 128


FLOOR_SCORE = -1e30


def shifted(block, axis, distance):
    devices = range(lax.axis_size(axis))
    route = [(i - distance, i) for i in devices if i - distance in devices]
    return lax.ppermute(block, axis, route)


def rotated(block, axis, distance):
    count = lax.axis_size(axis)
    route = [(i, (i + distance) % count) for i in range(count)]
    return lax.ppermute(block, axis, route)


def attention(queries, keyvals, documents):
    length = queries.shape[1]
    pair_width = keyvals.shape[3]
    pair_heads = pair_width // HEAD_DIM
    query_group_size = queries.shape[2] // pair_width
    cycle_size = lax.axis_size("ctx")
    position = lax.axis_index("ctx")
    offsets = jnp.arange(length, dtype=jnp.int32)
    reach_hops = min(cycle_size - 1, (cycle_size * length // 2 - 1 + length - 1) // length)

    pair_blocks = [keyvals[0]]
    label_blocks = [documents[0]]
    place_blocks = [position * length + offsets]
    label_slab = jnp.broadcast_to(
        documents[0].astype(jnp.bfloat16)[:, None, None], (length, 1, pair_width)
    )
    packed = jnp.concatenate([keyvals[0], label_slab], axis=1)
    for hop in range(1, reach_hops + 1):
        arrived = shifted(packed, "ctx", hop)
        pair_blocks.append(arrived[:, :2])
        label_blocks.append(arrived[:, 2, 0].astype(jnp.int32))
        place_blocks.append((position - hop) * length + offsets)
    pairs = jnp.concatenate(pair_blocks, axis=0)
    key_labels = jnp.concatenate(label_blocks, axis=0)
    key_place = jnp.concatenate(place_blocks, axis=0)
    key_count = pairs.shape[0]

    query_place = position * length + offsets
    query_labels = documents[0]
    query_block = queries[0].reshape(length, pair_heads, query_group_size, HEAD_DIM)
    key_block = pairs[:, 0].reshape(key_count, pair_heads, HEAD_DIM)
    value_block = pairs[:, 1].reshape(key_count, pair_heads, HEAD_DIM)

    scores = jnp.einsum(
        "qhgd,khd->hgqk", query_block, key_block, preferred_element_type=jnp.float32
    )
    scores = scores * (1.0 / math.sqrt(HEAD_DIM))
    allowed = (
        (query_labels[:, None] == key_labels[None, :])
        & (key_place[None, :] <= query_place[:, None])
        & (key_place[None, :] >= 0)
    )
    scores = jnp.where(allowed, scores, FLOOR_SCORE)
    peak = jnp.max(scores, axis=-1, keepdims=True)
    expo = jnp.where(allowed, jnp.exp(scores - peak), 0.0)
    total = jnp.sum(expo, axis=-1)
    summed = jnp.einsum(
        "hgqk,khd->qhgd",
        expo.astype(jnp.bfloat16),
        value_block,
        preferred_element_type=jnp.float32,
    )
    head_values = summed / jnp.transpose(total, (2, 0, 1))[..., None]
    return head_values.reshape(length, pair_heads * query_group_size * HEAD_DIM).astype(
        jnp.bfloat16
    )


def swapped(block, axis):
    return lax.ppermute(block, axis, [(0, 1), (1, 0)])


def sent(block, route):
    return lax.ppermute(block, ("dp", "tensor"), route)


def needed_heads(head_values):
    group = lax.axis_size("tensor")
    me = lax.axis_index("tensor")
    side = lax.axis_index("dp")
    foreign = swapped(head_values, "dp")
    mine = jnp.concatenate([head_values, foreign], axis=1)
    owners = [(s, 2 * s + k) for s in range(2) for k in range(2)]
    over_y = sent(mine, [(s * group + p, s * group + (p ^ 2)) for s, p in owners])
    beside = sent(mine, [(s * group + p, s * group + (p ^ 1)) for s, p in owners])
    relayed = sent(
        over_y, [(s * group + (p ^ 2), s * group + (p ^ 3)) for s, p in owners]
    )
    on_owner = me // 2 == side
    same_core = jnp.where(on_owner, mine, over_y)
    other_core = jnp.where(on_owner, beside, relayed)
    first_core = me % 2 == 0
    width = head_values.shape[1]
    lower = jnp.where(first_core, same_core, other_core)
    upper = jnp.where(first_core, other_core, same_core)
    own_full = jnp.concatenate([lower[:, :width], upper[:, :width]], axis=1)
    foreign_full = jnp.concatenate([lower[:, width:], upper[:, width:]], axis=1)
    return own_full, foreign_full


def first_hop(block, axis):
    count = lax.axis_size(axis)
    rising = lax.ppermute(block, axis, [(i, i + 1) for i in range(count - 1)])
    falling = lax.ppermute(block, axis, [(i, i - 1) for i in range(1, count)])
    return rising, falling


def line_rows(block, first, axis):
    count = lax.axis_size(axis)
    here = lax.axis_index(axis)
    rising, falling = first
    arrivals = [(block, 0), (rising, -1), (falling, 1)]
    for step in range(2, count):
        rising = lax.ppermute(rising, axis, [(i, i + 1) for i in range(step - 1, count - 1)])
        falling = lax.ppermute(falling, axis, [(i, i - 1) for i in range(1, count - step + 1)])
        arrivals.append((rising, -step))
        arrivals.append((falling, step))
    ordered = []
    for place in range(count):
        chosen = jnp.zeros_like(block)
        for arrived, offset in arrivals:
            chosen = jnp.where(here + offset == place, arrived, chosen)
        ordered.append(chosen)
    return jnp.concatenate(ordered, axis=0)


def split_projection(head_values, side_rows):
    own_full, foreign_full = needed_heads(head_values)
    returned = []
    for rows in side_rows:
        partner = jnp.dot(foreign_full, rows, preferred_element_type=jnp.float32)
        returned.append(swapped(partner.astype(jnp.bfloat16), "dp"))
    own_full, side_rows = lax.optimization_barrier((own_full, side_rows))
    outputs = []
    for rows, back in zip(side_rows, returned):
        local = jnp.dot(own_full, rows, preferred_element_type=jnp.float32)
        local = lax.optimization_barrier(local)
        outputs.append(local + back.astype(jnp.float32))
    return jnp.concatenate(outputs, axis=1)


def shards(queries, keyvals, documents, output_weight):
    block_rows = output_weight.shape[0]
    width = queries.shape[2]
    side_width = block_rows * lax.axis_size("ctx")
    fits = lax.axis_size("tensor") == 4 and output_weight.shape[1] % 256 == 0
    if lax.axis_size("dp") == 2 and side_width == 2 * width and fits:
        half = output_weight.shape[1] // 2
        halves = [output_weight[:, :half], output_weight[:, half:]]
        firsts = [first_hop(piece, "ctx") for piece in halves]
        head_values = attention(queries, keyvals, documents)
        firsts, head_values = lax.optimization_barrier((firsts, head_values))
        side_rows = [line_rows(piece, f, "ctx") for piece, f in zip(halves, firsts)]
        result = split_projection(head_values, side_rows)
        return result.astype(jnp.bfloat16)[None]
    all_rows = lax.all_gather(output_weight, ("dp", "ctx"), axis=0, tiled=True)
    head_values = attention(queries, keyvals, documents)
    group = lax.axis_size("tensor")
    me = lax.axis_index("tensor")
    result = None
    for distance in range(group):
        held = head_values if distance == 0 else rotated(head_values, "tensor", distance)
        owner = (me - distance) % group
        rows = lax.dynamic_slice_in_dim(all_rows, owner * width, width, 0)
        part = jnp.dot(held, rows, preferred_element_type=jnp.float32)
        result = part if result is None else result + part
    return result.astype(jnp.bfloat16)[None]


def solution(mesh):
    placed = (
        P("dp", "ctx", "tensor"),
        P("dp", "ctx", None, "tensor"),
        P("dp", "ctx"),
        P(("dp", "ctx"), "tensor"),
    )
    return jax.shard_map(
        shards, mesh=mesh, in_specs=placed, out_specs=P("dp", "ctx", "tensor"), check_vma=False
    )
```

```python
import math

import jax
import jax.numpy as jnp
from jax import lax
from jax.sharding import PartitionSpec as P

HEAD_DIM = 128


FLOOR_SCORE = -1e30


def shifted(block, axis, distance):
    devices = range(lax.axis_size(axis))
    route = [(i - distance, i) for i in devices if i - distance in devices]
    return lax.ppermute(block, axis, route)


def rotated(block, axis, distance):
    count = lax.axis_size(axis)
    route = [(i, (i + distance) % count) for i in range(count)]
    return lax.ppermute(block, axis, route)


def attention(queries, keyvals, documents):
    length = queries.shape[1]
    pair_width = keyvals.shape[3]
    pair_heads = pair_width // HEAD_DIM
    query_group_size = queries.shape[2] // pair_width
    cycle_size = lax.axis_size("ctx")
    position = lax.axis_index("ctx")
    offsets = jnp.arange(length, dtype=jnp.int32)
    reach_hops = min(cycle_size - 1, (cycle_size * length // 2 - 1 + length - 1) // length)

    pair_blocks = [keyvals[0]]
    label_blocks = [documents[0]]
    place_blocks = [position * length + offsets]
    label_slab = jnp.broadcast_to(
        documents[0].astype(jnp.bfloat16)[:, None, None], (length, 1, pair_width)
    )
    packed = jnp.concatenate([keyvals[0], label_slab], axis=1)
    for hop in range(1, reach_hops + 1):
        arrived = shifted(packed, "ctx", hop)
        pair_blocks.append(arrived[:, :2])
        label_blocks.append(arrived[:, 2, 0].astype(jnp.int32))
        place_blocks.append((position - hop) * length + offsets)
    pairs = jnp.concatenate(pair_blocks, axis=0)
    key_labels = jnp.concatenate(label_blocks, axis=0)
    key_place = jnp.concatenate(place_blocks, axis=0)
    key_count = pairs.shape[0]

    query_place = position * length + offsets
    query_labels = documents[0]
    query_block = queries[0].reshape(length, pair_heads, query_group_size, HEAD_DIM)
    key_block = pairs[:, 0].reshape(key_count, pair_heads, HEAD_DIM)
    value_block = pairs[:, 1].reshape(key_count, pair_heads, HEAD_DIM)

    scores = jnp.einsum(
        "qhgd,khd->hgqk", query_block, key_block, preferred_element_type=jnp.float32
    )
    scores = scores * (1.0 / math.sqrt(HEAD_DIM))
    allowed = (
        (query_labels[:, None] == key_labels[None, :])
        & (key_place[None, :] <= query_place[:, None])
        & (key_place[None, :] >= 0)
    )
    scores = jnp.where(allowed, scores, FLOOR_SCORE)
    peak = jnp.max(scores, axis=-1, keepdims=True)
    expo = jnp.where(allowed, jnp.exp(scores - peak), 0.0)
    total = jnp.sum(expo, axis=-1)
    summed = jnp.einsum(
        "hgqk,khd->qhgd",
        expo.astype(jnp.bfloat16),
        value_block,
        preferred_element_type=jnp.float32,
    )
    head_values = summed / jnp.transpose(total, (2, 0, 1))[..., None]
    return head_values.reshape(length, pair_heads * query_group_size * HEAD_DIM).astype(
        jnp.bfloat16
    )


def swapped(block, axis):
    return lax.ppermute(block, axis, [(0, 1), (1, 0)])


def sent(block, route):
    return lax.ppermute(block, ("dp", "tensor"), route)


def needed_heads(head_values):
    group = lax.axis_size("tensor")
    me = lax.axis_index("tensor")
    side = lax.axis_index("dp")
    foreign = swapped(head_values, "dp")
    mine = jnp.concatenate([head_values, foreign], axis=1)
    owners = [(s, 2 * s + k) for s in range(2) for k in range(2)]
    over_y = sent(mine, [(s * group + p, s * group + (p ^ 2)) for s, p in owners])
    beside = sent(mine, [(s * group + p, s * group + (p ^ 1)) for s, p in owners])
    relayed = sent(
        over_y, [(s * group + (p ^ 2), s * group + (p ^ 3)) for s, p in owners]
    )
    on_owner = me // 2 == side
    same_core = jnp.where(on_owner, mine, over_y)
    other_core = jnp.where(on_owner, beside, relayed)
    first_core = me % 2 == 0
    width = head_values.shape[1]
    lower = jnp.where(first_core, same_core, other_core)
    upper = jnp.where(first_core, other_core, same_core)
    own_full = jnp.concatenate([lower[:, :width], upper[:, :width]], axis=1)
    foreign_full = jnp.concatenate([lower[:, width:], upper[:, width:]], axis=1)
    return own_full, foreign_full


def ring_step(block, axis):
    count = lax.axis_size(axis)
    return lax.ppermute(block, axis, [(i, (i + 1) % count) for i in range(count)])


def line_rows(block, first, axis):
    count = lax.axis_size(axis)
    here = lax.axis_index(axis)
    arrivals = [(block, 0), (first, 1)]
    carried = first
    for step in range(2, count):
        carried = ring_step(carried, axis)
        arrivals.append((carried, step))
    ordered = []
    for place in range(count):
        chosen = jnp.zeros_like(block)
        for arrived, back in arrivals:
            chosen = jnp.where((here - back) % count == place, arrived, chosen)
        ordered.append(chosen)
    return jnp.concatenate(ordered, axis=0)


def split_projection(head_values, side_rows):
    own_full, foreign_full = needed_heads(head_values)
    partner = jnp.dot(foreign_full, side_rows, preferred_element_type=jnp.float32)
    outgoing = partner.astype(jnp.bfloat16)
    returned = swapped(outgoing, "dp")
    outgoing, own_full, side_rows = lax.optimization_barrier((outgoing, own_full, side_rows))
    local = jnp.dot(own_full, side_rows, preferred_element_type=jnp.float32)
    local = lax.optimization_barrier(local)
    return local + returned.astype(jnp.float32)


def shards(queries, keyvals, documents, output_weight):
    block_rows = output_weight.shape[0]
    width = queries.shape[2]
    side_width = block_rows * lax.axis_size("ctx")
    fits = lax.axis_size("tensor") == 4
    if lax.axis_size("dp") == 2 and side_width == 2 * width and fits:
        first = ring_step(output_weight, "ctx")
        head_values = attention(queries, keyvals, documents)
        first, head_values = lax.optimization_barrier((first, head_values))
        side_rows = line_rows(output_weight, first, "ctx")
        result = split_projection(head_values, side_rows)
        return result.astype(jnp.bfloat16)[None]
    all_rows = lax.all_gather(output_weight, ("dp", "ctx"), axis=0, tiled=True)
    head_values = attention(queries, keyvals, documents)
    group = lax.axis_size("tensor")
    me = lax.axis_index("tensor")
    result = None
    for distance in range(group):
        held = head_values if distance == 0 else rotated(head_values, "tensor", distance)
        owner = (me - distance) % group
        rows = lax.dynamic_slice_in_dim(all_rows, owner * width, width, 0)
        part = jnp.dot(held, rows, preferred_element_type=jnp.float32)
        result = part if result is None else result + part
    return result.astype(jnp.bfloat16)[None]


def solution(mesh):
    placed = (
        P("dp", "ctx", "tensor"),
        P("dp", "ctx", None, "tensor"),
        P("dp", "ctx"),
        P(("dp", "ctx"), "tensor"),
    )
    return jax.shard_map(
        shards, mesh=mesh, in_specs=placed, out_specs=P("dp", "ctx", "tensor"), check_vma=False
    )
```

```python
import math

import jax
import jax.numpy as jnp
from jax import lax
from jax.sharding import PartitionSpec as P

HEAD_DIM = 128


FLOOR_SCORE = -1e30


def shifted(block, axis, distance):
    devices = range(lax.axis_size(axis))
    route = [(i - distance, i) for i in devices if i - distance in devices]
    return lax.ppermute(block, axis, route)


def rotated(block, axis, distance):
    count = lax.axis_size(axis)
    route = [(i, (i + distance) % count) for i in range(count)]
    return lax.ppermute(block, axis, route)


def attention(queries, keyvals, documents):
    length = queries.shape[1]
    pair_width = keyvals.shape[3]
    pair_heads = pair_width // HEAD_DIM
    query_group_size = queries.shape[2] // pair_width
    cycle_size = lax.axis_size("ctx")
    position = lax.axis_index("ctx")
    offsets = jnp.arange(length, dtype=jnp.int32)
    reach_hops = min(cycle_size - 1, (cycle_size * length // 2 - 1 + length - 1) // length)

    pair_blocks = [keyvals[0]]
    label_blocks = [documents[0]]
    place_blocks = [position * length + offsets]
    label_slab = jnp.broadcast_to(
        documents[0].astype(jnp.bfloat16)[:, None, None], (length, 1, pair_width)
    )
    packed = jnp.concatenate([keyvals[0], label_slab], axis=1)
    for hop in range(1, reach_hops + 1):
        arrived = shifted(packed, "ctx", hop)
        pair_blocks.append(arrived[:, :2])
        label_blocks.append(arrived[:, 2, 0].astype(jnp.int32))
        place_blocks.append((position - hop) * length + offsets)
    pairs = jnp.concatenate(pair_blocks, axis=0)
    key_labels = jnp.concatenate(label_blocks, axis=0)
    key_place = jnp.concatenate(place_blocks, axis=0)
    key_count = pairs.shape[0]

    query_place = position * length + offsets
    query_labels = documents[0]
    query_block = queries[0].reshape(length, pair_heads, query_group_size, HEAD_DIM)
    key_block = pairs[:, 0].reshape(key_count, pair_heads, HEAD_DIM)
    value_block = pairs[:, 1].reshape(key_count, pair_heads, HEAD_DIM)

    scores = jnp.einsum(
        "qhgd,khd->hgqk", query_block, key_block, preferred_element_type=jnp.float32
    )
    scores = scores * (1.0 / math.sqrt(HEAD_DIM))
    allowed = (
        (query_labels[:, None] == key_labels[None, :])
        & (key_place[None, :] <= query_place[:, None])
        & (key_place[None, :] >= 0)
    )
    scores = jnp.where(allowed, scores, FLOOR_SCORE)
    peak = jnp.max(scores, axis=-1, keepdims=True)
    expo = jnp.where(allowed, jnp.exp(scores - peak), 0.0)
    total = jnp.sum(expo, axis=-1)
    summed = jnp.einsum(
        "hgqk,khd->qhgd",
        expo.astype(jnp.bfloat16),
        value_block,
        preferred_element_type=jnp.float32,
    )
    head_values = summed / jnp.transpose(total, (2, 0, 1))[..., None]
    return head_values.reshape(length, pair_heads * query_group_size * HEAD_DIM).astype(
        jnp.bfloat16
    )


def swapped(block, axis):
    return lax.ppermute(block, axis, [(0, 1), (1, 0)])


def sent(block, route):
    return lax.ppermute(block, ("dp", "tensor"), route)


def needed_heads(head_values):
    group = lax.axis_size("tensor")
    me = lax.axis_index("tensor")
    side = lax.axis_index("dp")
    foreign = swapped(head_values, "dp")
    mine = jnp.concatenate([head_values, foreign], axis=1)
    owners = [(s, 2 * s + k) for s in range(2) for k in range(2)]
    over_y = sent(mine, [(s * group + p, s * group + (p ^ 2)) for s, p in owners])
    on_owner = me // 2 == side
    same_core = jnp.where(on_owner, mine, over_y)
    other_core = lax.ppermute(same_core, "tensor", [(t, t ^ 1) for t in range(group)])
    first_core = me % 2 == 0
    width = head_values.shape[1]
    lower = jnp.where(first_core, same_core, other_core)
    upper = jnp.where(first_core, other_core, same_core)
    own_full = jnp.concatenate([lower[:, :width], upper[:, :width]], axis=1)
    foreign_full = jnp.concatenate([lower[:, width:], upper[:, width:]], axis=1)
    return own_full, foreign_full


def ring_step(block, axis):
    count = lax.axis_size(axis)
    return lax.ppermute(block, axis, [(i, (i + 1) % count) for i in range(count)])


def line_rows(block, first, axis):
    count = lax.axis_size(axis)
    here = lax.axis_index(axis)
    arrivals = [(block, 0), (first, 1)]
    carried = first
    for step in range(2, count):
        carried = ring_step(carried, axis)
        arrivals.append((carried, step))
    ordered = []
    for place in range(count):
        chosen = jnp.zeros_like(block)
        for arrived, back in arrivals:
            chosen = jnp.where((here - back) % count == place, arrived, chosen)
        ordered.append(chosen)
    return jnp.concatenate(ordered, axis=0)


def split_projection(head_values, side_rows):
    own_full, foreign_full = needed_heads(head_values)
    partner = jnp.dot(foreign_full, side_rows, preferred_element_type=jnp.float32)
    outgoing = partner.astype(jnp.bfloat16)
    returned = swapped(outgoing, "dp")
    outgoing, own_full, side_rows = lax.optimization_barrier((outgoing, own_full, side_rows))
    local = jnp.dot(own_full, side_rows, preferred_element_type=jnp.float32)
    local = lax.optimization_barrier(local)
    return local + returned.astype(jnp.float32)


def shards(queries, keyvals, documents, output_weight):
    block_rows = output_weight.shape[0]
    width = queries.shape[2]
    side_width = block_rows * lax.axis_size("ctx")
    fits = lax.axis_size("tensor") == 4
    if lax.axis_size("dp") == 2 and side_width == 2 * width and fits:
        first = ring_step(output_weight, "ctx")
        head_values = attention(queries, keyvals, documents)
        first, head_values = lax.optimization_barrier((first, head_values))
        side_rows = line_rows(output_weight, first, "ctx")
        result = split_projection(head_values, side_rows)
        return result.astype(jnp.bfloat16)[None]
    all_rows = lax.all_gather(output_weight, ("dp", "ctx"), axis=0, tiled=True)
    head_values = attention(queries, keyvals, documents)
    group = lax.axis_size("tensor")
    me = lax.axis_index("tensor")
    result = None
    for distance in range(group):
        held = head_values if distance == 0 else rotated(head_values, "tensor", distance)
        owner = (me - distance) % group
        rows = lax.dynamic_slice_in_dim(all_rows, owner * width, width, 0)
        part = jnp.dot(held, rows, preferred_element_type=jnp.float32)
        result = part if result is None else result + part
    return result.astype(jnp.bfloat16)[None]


def solution(mesh):
    placed = (
        P("dp", "ctx", "tensor"),
        P("dp", "ctx", None, "tensor"),
        P("dp", "ctx"),
        P(("dp", "ctx"), "tensor"),
    )
    return jax.shard_map(
        shards, mesh=mesh, in_specs=placed, out_specs=P("dp", "ctx", "tensor"), check_vma=False
    )
```

```python
import math

import jax
import jax.numpy as jnp
from jax import lax
from jax.sharding import PartitionSpec as P

HEAD_DIM = 128


FLOOR_SCORE = -1e30


def shifted(block, axis, distance):
    devices = range(lax.axis_size(axis))
    route = [(i - distance, i) for i in devices if i - distance in devices]
    return lax.ppermute(block, axis, route)


def rotated(block, axis, distance):
    count = lax.axis_size(axis)
    route = [(i, (i + distance) % count) for i in range(count)]
    return lax.ppermute(block, axis, route)


def attention(queries, keyvals, documents, anchor):
    length = queries.shape[1]
    pair_width = keyvals.shape[3]
    pair_heads = pair_width // HEAD_DIM
    query_group_size = queries.shape[2] // pair_width
    cycle_size = lax.axis_size("ctx")
    position = lax.axis_index("ctx")
    offsets = jnp.arange(length, dtype=jnp.int32)
    reach_hops = min(cycle_size - 1, (cycle_size * length // 2 - 1 + length - 1) // length)

    pair_blocks = [keyvals[0]]
    label_blocks = [documents[0]]
    place_blocks = [position * length + offsets]
    label_slab = jnp.broadcast_to(
        documents[0].astype(jnp.bfloat16)[:, None, None], (length, 1, pair_width)
    )
    packed = jnp.concatenate([keyvals[0], label_slab], axis=1)
    for hop in range(1, reach_hops + 1):
        arrived = shifted(packed, "ctx", hop)
        pair_blocks.append(arrived[:, :2])
        label_blocks.append(arrived[:, 2, 0].astype(jnp.int32))
        place_blocks.append((position - hop) * length + offsets)
    pairs = jnp.concatenate(pair_blocks, axis=0)
    pairs, anchor = lax.optimization_barrier((pairs, anchor))
    key_labels = jnp.concatenate(label_blocks, axis=0)
    key_place = jnp.concatenate(place_blocks, axis=0)
    key_count = pairs.shape[0]

    query_place = position * length + offsets
    query_labels = documents[0]
    query_block = queries[0].reshape(length, pair_heads, query_group_size, HEAD_DIM)
    key_block = pairs[:, 0].reshape(key_count, pair_heads, HEAD_DIM)
    value_block = pairs[:, 1].reshape(key_count, pair_heads, HEAD_DIM)

    scores = jnp.einsum(
        "qhgd,khd->hgqk", query_block, key_block, preferred_element_type=jnp.float32
    )
    scores = scores * (1.0 / math.sqrt(HEAD_DIM))
    allowed = (
        (query_labels[:, None] == key_labels[None, :])
        & (key_place[None, :] <= query_place[:, None])
        & (key_place[None, :] >= 0)
    )
    scores = jnp.where(allowed, scores, FLOOR_SCORE)
    peak = jnp.max(scores, axis=-1, keepdims=True)
    expo = jnp.where(allowed, jnp.exp(scores - peak), 0.0)
    total = jnp.sum(expo, axis=-1)
    summed = jnp.einsum(
        "hgqk,khd->qhgd",
        expo.astype(jnp.bfloat16),
        value_block,
        preferred_element_type=jnp.float32,
    )
    head_values = summed / jnp.transpose(total, (2, 0, 1))[..., None]
    head_values = head_values.reshape(length, pair_heads * query_group_size * HEAD_DIM)
    return head_values.astype(jnp.bfloat16), anchor


def swapped(block, axis):
    return lax.ppermute(block, axis, [(0, 1), (1, 0)])


def sent(block, route):
    return lax.ppermute(block, ("dp", "tensor"), route)


def needed_heads(head_values):
    group = lax.axis_size("tensor")
    me = lax.axis_index("tensor")
    side = lax.axis_index("dp")
    foreign = swapped(head_values, "dp")
    mine = jnp.concatenate([head_values, foreign], axis=1)
    owners = [(s, 2 * s + k) for s in range(2) for k in range(2)]
    over_y = sent(mine, [(s * group + p, s * group + (p ^ 2)) for s, p in owners])
    beside = sent(mine, [(s * group + p, s * group + (p ^ 1)) for s, p in owners])
    relayed = sent(
        over_y, [(s * group + (p ^ 2), s * group + (p ^ 3)) for s, p in owners]
    )
    on_owner = me // 2 == side
    same_core = jnp.where(on_owner, mine, over_y)
    other_core = jnp.where(on_owner, beside, relayed)
    first_core = me % 2 == 0
    width = head_values.shape[1]
    lower = jnp.where(first_core, same_core, other_core)
    upper = jnp.where(first_core, other_core, same_core)
    own_full = jnp.concatenate([lower[:, :width], upper[:, :width]], axis=1)
    foreign_full = jnp.concatenate([lower[:, width:], upper[:, width:]], axis=1)
    return own_full, foreign_full


def ring_step(block, axis):
    count = lax.axis_size(axis)
    return lax.ppermute(block, axis, [(i, (i + 1) % count) for i in range(count)])


def line_rows(block, first, axis):
    count = lax.axis_size(axis)
    here = lax.axis_index(axis)
    arrivals = [(block, 0), (first, 1)]
    carried = first
    for step in range(2, count):
        carried = ring_step(carried, axis)
        arrivals.append((carried, step))
    ordered = []
    for place in range(count):
        chosen = jnp.zeros_like(block)
        for arrived, back in arrivals:
            chosen = jnp.where((here - back) % count == place, arrived, chosen)
        ordered.append(chosen)
    return jnp.concatenate(ordered, axis=0)


def split_projection(head_values, side_rows):
    own_full, foreign_full = needed_heads(head_values)
    partner = jnp.dot(foreign_full, side_rows, preferred_element_type=jnp.float32)
    outgoing = partner.astype(jnp.bfloat16)
    returned = swapped(outgoing, "dp")
    outgoing, own_full, side_rows = lax.optimization_barrier((outgoing, own_full, side_rows))
    local = jnp.dot(own_full, side_rows, preferred_element_type=jnp.float32)
    local = lax.optimization_barrier(local)
    return local + returned.astype(jnp.float32)


def shards(queries, keyvals, documents, output_weight):
    block_rows = output_weight.shape[0]
    width = queries.shape[2]
    side_width = block_rows * lax.axis_size("ctx")
    fits = lax.axis_size("tensor") == 4
    if lax.axis_size("dp") == 2 and side_width == 2 * width and fits:
        first = ring_step(output_weight, "ctx")
        head_values, first = attention(queries, keyvals, documents, first)
        side_rows = line_rows(output_weight, first, "ctx")
        result = split_projection(head_values, side_rows)
        return result.astype(jnp.bfloat16)[None]
    all_rows = lax.all_gather(output_weight, ("dp", "ctx"), axis=0, tiled=True)
    head_values, _ = attention(queries, keyvals, documents, ())
    group = lax.axis_size("tensor")
    me = lax.axis_index("tensor")
    result = None
    for distance in range(group):
        held = head_values if distance == 0 else rotated(head_values, "tensor", distance)
        owner = (me - distance) % group
        rows = lax.dynamic_slice_in_dim(all_rows, owner * width, width, 0)
        part = jnp.dot(held, rows, preferred_element_type=jnp.float32)
        result = part if result is None else result + part
    return result.astype(jnp.bfloat16)[None]


def solution(mesh):
    placed = (
        P("dp", "ctx", "tensor"),
        P("dp", "ctx", None, "tensor"),
        P("dp", "ctx"),
        P(("dp", "ctx"), "tensor"),
    )
    return jax.shard_map(
        shards, mesh=mesh, in_specs=placed, out_specs=P("dp", "ctx", "tensor"), check_vma=False
    )
```

```python
import math

import jax
import jax.numpy as jnp
from jax import lax
from jax.sharding import PartitionSpec as P

HEAD_DIM = 128


FLOOR_SCORE = -1e30


def shifted(block, axis, distance):
    devices = range(lax.axis_size(axis))
    route = [(i - distance, i) for i in devices if i - distance in devices]
    return lax.ppermute(block, axis, route)


def rotated(block, axis, distance):
    count = lax.axis_size(axis)
    route = [(i, (i + distance) % count) for i in range(count)]
    return lax.ppermute(block, axis, route)


def attention(queries, keyvals, documents):
    length = queries.shape[1]
    pair_width = keyvals.shape[3]
    pair_heads = pair_width // HEAD_DIM
    query_group_size = queries.shape[2] // pair_width
    cycle_size = lax.axis_size("ctx")
    position = lax.axis_index("ctx")
    offsets = jnp.arange(length, dtype=jnp.int32)
    reach_hops = min(cycle_size - 1, (cycle_size * length // 2 - 1 + length - 1) // length)

    pair_blocks = [keyvals[0]]
    label_blocks = [documents[0]]
    place_blocks = [position * length + offsets]
    label_slab = jnp.broadcast_to(
        documents[0].astype(jnp.bfloat16)[:, None, None], (length, 1, pair_width)
    )
    packed = jnp.concatenate([keyvals[0], label_slab], axis=1)
    for hop in range(1, reach_hops + 1):
        arrived = shifted(packed, "ctx", hop)
        pair_blocks.append(arrived[:, :2])
        label_blocks.append(arrived[:, 2, 0].astype(jnp.int32))
        place_blocks.append((position - hop) * length + offsets)
    pairs = jnp.concatenate(pair_blocks, axis=0)
    key_labels = jnp.concatenate(label_blocks, axis=0)
    key_place = jnp.concatenate(place_blocks, axis=0)
    key_count = pairs.shape[0]

    query_place = position * length + offsets
    query_labels = documents[0]
    query_block = queries[0].reshape(length, pair_heads, query_group_size, HEAD_DIM)
    key_block = pairs[:, 0].reshape(key_count, pair_heads, HEAD_DIM)
    value_block = pairs[:, 1].reshape(key_count, pair_heads, HEAD_DIM)

    scores = jnp.einsum(
        "qhgd,khd->hgqk", query_block, key_block, preferred_element_type=jnp.float32
    )
    scores = scores * (1.0 / math.sqrt(HEAD_DIM))
    allowed = (
        (query_labels[:, None] == key_labels[None, :])
        & (key_place[None, :] <= query_place[:, None])
        & (key_place[None, :] >= 0)
    )
    scores = jnp.where(allowed, scores, FLOOR_SCORE)
    peak = jnp.max(scores, axis=-1, keepdims=True)
    expo = jnp.where(allowed, jnp.exp(scores - peak), 0.0)
    total = jnp.sum(expo, axis=-1)
    summed = jnp.einsum(
        "hgqk,khd->qhgd",
        expo.astype(jnp.bfloat16),
        value_block,
        preferred_element_type=jnp.float32,
    )
    head_values = summed / jnp.transpose(total, (2, 0, 1))[..., None]
    return head_values.reshape(length, pair_heads * query_group_size * HEAD_DIM).astype(
        jnp.bfloat16
    )


def swapped(block, axis):
    return lax.ppermute(block, axis, [(0, 1), (1, 0)])


def sent(block, route):
    return lax.ppermute(block, ("dp", "tensor"), route)


def needed_heads(head_values):
    group = lax.axis_size("tensor")
    me = lax.axis_index("tensor")
    side = lax.axis_index("dp")
    width = head_values.shape[1]
    foreign = swapped(head_values, "dp")
    owners = [(s, 2 * s + k) for s in range(2) for k in range(2)]
    own_over = sent(head_values, [(s * group + p, s * group + (p ^ 2)) for s, p in owners])
    diagonal = [((1 - s) * group + p, s * group + (p ^ 2)) for s, p in owners]
    foreign_over = sent(head_values, diagonal)
    on_owner = me // 2 == side
    own_same = jnp.where(on_owner, head_values, own_over)
    foreign_same = jnp.where(on_owner, foreign, foreign_over)
    same_core = jnp.concatenate([own_same, foreign_same], axis=1)
    other_core = lax.ppermute(same_core, "tensor", [(t, t ^ 1) for t in range(group)])
    first_core = me % 2 == 0
    lower = jnp.where(first_core, same_core, other_core)
    upper = jnp.where(first_core, other_core, same_core)
    own_full = jnp.concatenate([lower[:, :width], upper[:, :width]], axis=1)
    foreign_full = jnp.concatenate([lower[:, width:], upper[:, width:]], axis=1)
    return own_full, foreign_full


def ring_step(block, axis):
    count = lax.axis_size(axis)
    return lax.ppermute(block, axis, [(i, (i + 1) % count) for i in range(count)])


def line_rows(block, first, axis):
    count = lax.axis_size(axis)
    here = lax.axis_index(axis)
    arrivals = [(block, 0), (first, 1)]
    carried = first
    for step in range(2, count):
        carried = ring_step(carried, axis)
        arrivals.append((carried, step))
    ordered = []
    for place in range(count):
        chosen = jnp.zeros_like(block)
        for arrived, back in arrivals:
            chosen = jnp.where((here - back) % count == place, arrived, chosen)
        ordered.append(chosen)
    return jnp.concatenate(ordered, axis=0)


def split_projection(head_values, side_rows):
    own_full, foreign_full = needed_heads(head_values)
    partner = jnp.dot(foreign_full, side_rows, preferred_element_type=jnp.float32)
    outgoing = partner.astype(jnp.bfloat16)
    returned = swapped(outgoing, "dp")
    outgoing, own_full, side_rows = lax.optimization_barrier((outgoing, own_full, side_rows))
    local = jnp.dot(own_full, side_rows, preferred_element_type=jnp.float32)
    local = lax.optimization_barrier(local)
    return local + returned.astype(jnp.float32)


def shards(queries, keyvals, documents, output_weight):
    block_rows = output_weight.shape[0]
    width = queries.shape[2]
    side_width = block_rows * lax.axis_size("ctx")
    fits = lax.axis_size("tensor") == 4
    if lax.axis_size("dp") == 2 and side_width == 2 * width and fits:
        first = ring_step(output_weight, "ctx")
        head_values = attention(queries, keyvals, documents)
        first, head_values = lax.optimization_barrier((first, head_values))
        side_rows = line_rows(output_weight, first, "ctx")
        result = split_projection(head_values, side_rows)
        return result.astype(jnp.bfloat16)[None]
    all_rows = lax.all_gather(output_weight, ("dp", "ctx"), axis=0, tiled=True)
    head_values = attention(queries, keyvals, documents)
    group = lax.axis_size("tensor")
    me = lax.axis_index("tensor")
    result = None
    for distance in range(group):
        held = head_values if distance == 0 else rotated(head_values, "tensor", distance)
        owner = (me - distance) % group
        rows = lax.dynamic_slice_in_dim(all_rows, owner * width, width, 0)
        part = jnp.dot(held, rows, preferred_element_type=jnp.float32)
        result = part if result is None else result + part
    return result.astype(jnp.bfloat16)[None]


def solution(mesh):
    placed = (
        P("dp", "ctx", "tensor"),
        P("dp", "ctx", None, "tensor"),
        P("dp", "ctx"),
        P(("dp", "ctx"), "tensor"),
    )
    return jax.shard_map(
        shards, mesh=mesh, in_specs=placed, out_specs=P("dp", "ctx", "tensor"), check_vma=False
    )
```

```python
import math

import jax
import jax.numpy as jnp
from jax import lax
from jax.sharding import PartitionSpec as P

HEAD_DIM = 128


FLOOR_SCORE = -1e30


def shifted(block, axis, distance):
    devices = range(lax.axis_size(axis))
    route = [(i - distance, i) for i in devices if i - distance in devices]
    return lax.ppermute(block, axis, route)


def rotated(block, axis, distance):
    count = lax.axis_size(axis)
    route = [(i, (i + distance) % count) for i in range(count)]
    return lax.ppermute(block, axis, route)


def attention(queries, keyvals, documents):
    length = queries.shape[1]
    pair_width = keyvals.shape[3]
    pair_heads = pair_width // HEAD_DIM
    query_group_size = queries.shape[2] // pair_width
    cycle_size = lax.axis_size("ctx")
    position = lax.axis_index("ctx")
    offsets = jnp.arange(length, dtype=jnp.int32)
    reach_hops = min(cycle_size - 1, (cycle_size * length // 2 - 1 + length - 1) // length)

    pair_blocks = [keyvals[0]]
    label_blocks = [documents[0]]
    place_blocks = [position * length + offsets]
    label_slab = jnp.broadcast_to(
        documents[0].astype(jnp.bfloat16)[:, None, None], (length, 1, pair_width)
    )
    packed = jnp.concatenate([keyvals[0], label_slab], axis=1)
    for hop in range(1, reach_hops + 1):
        arrived = shifted(packed, "ctx", hop)
        pair_blocks.append(arrived[:, :2])
        label_blocks.append(arrived[:, 2, 0].astype(jnp.int32))
        place_blocks.append((position - hop) * length + offsets)
    pairs = jnp.concatenate(pair_blocks, axis=0)
    key_labels = jnp.concatenate(label_blocks, axis=0)
    key_place = jnp.concatenate(place_blocks, axis=0)
    key_count = pairs.shape[0]

    query_place = position * length + offsets
    query_labels = documents[0]
    query_block = queries[0].reshape(length, pair_heads, query_group_size, HEAD_DIM)
    key_block = pairs[:, 0].reshape(key_count, pair_heads, HEAD_DIM)
    value_block = pairs[:, 1].reshape(key_count, pair_heads, HEAD_DIM)

    scores = jnp.einsum(
        "qhgd,khd->hgqk", query_block, key_block, preferred_element_type=jnp.float32
    )
    scores = scores * (1.0 / math.sqrt(HEAD_DIM))
    allowed = (
        (query_labels[:, None] == key_labels[None, :])
        & (key_place[None, :] <= query_place[:, None])
        & (key_place[None, :] >= 0)
    )
    scores = jnp.where(allowed, scores, FLOOR_SCORE)
    peak = jnp.max(scores, axis=-1, keepdims=True)
    expo = jnp.where(allowed, jnp.exp(scores - peak), 0.0)
    total = jnp.sum(expo, axis=-1)
    summed = jnp.einsum(
        "hgqk,khd->qhgd",
        expo.astype(jnp.bfloat16),
        value_block,
        preferred_element_type=jnp.float32,
    )
    head_values = summed / jnp.transpose(total, (2, 0, 1))[..., None]
    return head_values.reshape(length, pair_heads * query_group_size * HEAD_DIM).astype(
        jnp.bfloat16
    )


def swapped(block, axis):
    return lax.ppermute(block, axis, [(0, 1), (1, 0)])


def sent(block, route):
    return lax.ppermute(block, ("dp", "tensor"), route)


def needed_heads(head_values):
    group = lax.axis_size("tensor")
    me = lax.axis_index("tensor")
    side = lax.axis_index("dp")
    foreign = swapped(head_values, "dp")
    mine = jnp.concatenate([head_values, foreign], axis=1)
    owners = [(s, 2 * s + k) for s in range(2) for k in range(2)]
    over_y = sent(mine, [(s * group + p, s * group + (p ^ 2)) for s, p in owners])
    beside = sent(mine, [(s * group + p, s * group + (p ^ 1)) for s, p in owners])
    relayed = sent(
        over_y, [(s * group + (p ^ 2), s * group + (p ^ 3)) for s, p in owners]
    )
    on_owner = me // 2 == side
    same_core = jnp.where(on_owner, mine, over_y)
    other_core = jnp.where(on_owner, beside, relayed)
    first_core = me % 2 == 0
    width = head_values.shape[1]
    lower = jnp.where(first_core, same_core, other_core)
    upper = jnp.where(first_core, other_core, same_core)
    own_full = jnp.concatenate([lower[:, :width], upper[:, :width]], axis=1)
    foreign_full = jnp.concatenate([lower[:, width:], upper[:, width:]], axis=1)
    return own_full, foreign_full


def ring_step(block, axis):
    count = lax.axis_size(axis)
    return lax.ppermute(block, axis, [(i, (i - 1) % count) for i in range(count)])


def line_rows(block, first, axis):
    count = lax.axis_size(axis)
    here = lax.axis_index(axis)
    arrivals = [(block, 0), (first, 1)]
    carried = first
    for step in range(2, count):
        carried = ring_step(carried, axis)
        arrivals.append((carried, step))
    ordered = []
    for place in range(count):
        chosen = jnp.zeros_like(block)
        for arrived, back in arrivals:
            chosen = jnp.where((here + back) % count == place, arrived, chosen)
        ordered.append(chosen)
    return jnp.concatenate(ordered, axis=0)


def split_projection(head_values, side_rows):
    own_full, foreign_full = needed_heads(head_values)
    partner = jnp.dot(foreign_full, side_rows, preferred_element_type=jnp.float32)
    outgoing = partner.astype(jnp.bfloat16)
    returned = swapped(outgoing, "dp")
    outgoing, own_full, side_rows = lax.optimization_barrier((outgoing, own_full, side_rows))
    local = jnp.dot(own_full, side_rows, preferred_element_type=jnp.float32)
    local = lax.optimization_barrier(local)
    return local + returned.astype(jnp.float32)


def shards(queries, keyvals, documents, output_weight):
    block_rows = output_weight.shape[0]
    width = queries.shape[2]
    side_width = block_rows * lax.axis_size("ctx")
    fits = lax.axis_size("tensor") == 4
    if lax.axis_size("dp") == 2 and side_width == 2 * width and fits:
        first = ring_step(output_weight, "ctx")
        head_values = attention(queries, keyvals, documents)
        first, head_values = lax.optimization_barrier((first, head_values))
        side_rows = line_rows(output_weight, first, "ctx")
        result = split_projection(head_values, side_rows)
        return result.astype(jnp.bfloat16)[None]
    all_rows = lax.all_gather(output_weight, ("dp", "ctx"), axis=0, tiled=True)
    head_values = attention(queries, keyvals, documents)
    group = lax.axis_size("tensor")
    me = lax.axis_index("tensor")
    result = None
    for distance in range(group):
        held = head_values if distance == 0 else rotated(head_values, "tensor", distance)
        owner = (me - distance) % group
        rows = lax.dynamic_slice_in_dim(all_rows, owner * width, width, 0)
        part = jnp.dot(held, rows, preferred_element_type=jnp.float32)
        result = part if result is None else result + part
    return result.astype(jnp.bfloat16)[None]


def solution(mesh):
    placed = (
        P("dp", "ctx", "tensor"),
        P("dp", "ctx", None, "tensor"),
        P("dp", "ctx"),
        P(("dp", "ctx"), "tensor"),
    )
    return jax.shard_map(
        shards, mesh=mesh, in_specs=placed, out_specs=P("dp", "ctx", "tensor"), check_vma=False
    )
```

```python
import math

import jax
import jax.numpy as jnp
from jax import lax
from jax.sharding import PartitionSpec as P

HEAD_DIM = 128


FLOOR_SCORE = -1e30


def shifted(block, axis, distance):
    devices = range(lax.axis_size(axis))
    route = [(i - distance, i) for i in devices if i - distance in devices]
    return lax.ppermute(block, axis, route)


def rotated(block, axis, distance):
    count = lax.axis_size(axis)
    route = [(i, (i + distance) % count) for i in range(count)]
    return lax.ppermute(block, axis, route)


def attention(queries, keyvals, documents):
    length = queries.shape[1]
    pair_width = keyvals.shape[3]
    pair_heads = pair_width // HEAD_DIM
    query_group_size = queries.shape[2] // pair_width
    cycle_size = lax.axis_size("ctx")
    position = lax.axis_index("ctx")
    offsets = jnp.arange(length, dtype=jnp.int32)
    reach_hops = min(cycle_size - 1, (cycle_size * length // 2 - 1 + length - 1) // length)

    pair_blocks = [keyvals[0]]
    label_blocks = [documents[0]]
    place_blocks = [position * length + offsets]
    if length % pair_width == 0:
        label_rows = documents[0].astype(jnp.bfloat16).reshape(length // pair_width, pair_width)
        packed = jnp.concatenate([keyvals[0].reshape(2 * length, pair_width), label_rows], axis=0)
    else:
        label_slab = jnp.broadcast_to(
            documents[0].astype(jnp.bfloat16)[:, None, None], (length, 1, pair_width)
        )
        packed = jnp.concatenate([keyvals[0], label_slab], axis=1)
    for hop in range(1, reach_hops + 1):
        arrived = shifted(packed, "ctx", hop)
        if length % pair_width == 0:
            pair_blocks.append(arrived[: 2 * length].reshape(length, 2, pair_width))
            label_blocks.append(arrived[2 * length:].reshape(length).astype(jnp.int32))
        else:
            pair_blocks.append(arrived[:, :2])
            label_blocks.append(arrived[:, 2, 0].astype(jnp.int32))
        place_blocks.append((position - hop) * length + offsets)
    pairs = jnp.concatenate(pair_blocks, axis=0)
    key_labels = jnp.concatenate(label_blocks, axis=0)
    key_place = jnp.concatenate(place_blocks, axis=0)
    key_count = pairs.shape[0]

    query_place = position * length + offsets
    query_labels = documents[0]
    query_block = queries[0].reshape(length, pair_heads, query_group_size, HEAD_DIM)
    key_block = pairs[:, 0].reshape(key_count, pair_heads, HEAD_DIM)
    value_block = pairs[:, 1].reshape(key_count, pair_heads, HEAD_DIM)

    scores = jnp.einsum(
        "qhgd,khd->hgqk", query_block, key_block, preferred_element_type=jnp.float32
    )
    scores = scores * (1.0 / math.sqrt(HEAD_DIM))
    allowed = (
        (query_labels[:, None] == key_labels[None, :])
        & (key_place[None, :] <= query_place[:, None])
        & (key_place[None, :] >= 0)
    )
    scores = jnp.where(allowed, scores, FLOOR_SCORE)
    peak = jnp.max(scores, axis=-1, keepdims=True)
    expo = jnp.where(allowed, jnp.exp(scores - peak), 0.0)
    total = jnp.sum(expo, axis=-1)
    summed = jnp.einsum(
        "hgqk,khd->qhgd",
        expo.astype(jnp.bfloat16),
        value_block,
        preferred_element_type=jnp.float32,
    )
    head_values = summed / jnp.transpose(total, (2, 0, 1))[..., None]
    return head_values.reshape(length, pair_heads * query_group_size * HEAD_DIM).astype(
        jnp.bfloat16
    )


def swapped(block, axis):
    return lax.ppermute(block, axis, [(0, 1), (1, 0)])


def sent(block, route):
    return lax.ppermute(block, ("dp", "tensor"), route)


def needed_heads(head_values):
    group = lax.axis_size("tensor")
    me = lax.axis_index("tensor")
    side = lax.axis_index("dp")
    foreign = swapped(head_values, "dp")
    mine = jnp.concatenate([head_values, foreign], axis=1)
    owners = [(s, 2 * s + k) for s in range(2) for k in range(2)]
    over_y = sent(mine, [(s * group + p, s * group + (p ^ 2)) for s, p in owners])
    beside = sent(mine, [(s * group + p, s * group + (p ^ 1)) for s, p in owners])
    relayed = sent(
        over_y, [(s * group + (p ^ 2), s * group + (p ^ 3)) for s, p in owners]
    )
    on_owner = me // 2 == side
    same_core = jnp.where(on_owner, mine, over_y)
    other_core = jnp.where(on_owner, beside, relayed)
    first_core = me % 2 == 0
    width = head_values.shape[1]
    lower = jnp.where(first_core, same_core, other_core)
    upper = jnp.where(first_core, other_core, same_core)
    own_full = jnp.concatenate([lower[:, :width], upper[:, :width]], axis=1)
    foreign_full = jnp.concatenate([lower[:, width:], upper[:, width:]], axis=1)
    return own_full, foreign_full


def ring_step(block, axis):
    count = lax.axis_size(axis)
    return lax.ppermute(block, axis, [(i, (i + 1) % count) for i in range(count)])


def line_rows(block, first, axis):
    count = lax.axis_size(axis)
    here = lax.axis_index(axis)
    arrivals = [(block, 0), (first, 1)]
    carried = first
    for step in range(2, count):
        carried = ring_step(carried, axis)
        arrivals.append((carried, step))
    ordered = []
    for place in range(count):
        chosen = jnp.zeros_like(block)
        for arrived, back in arrivals:
            chosen = jnp.where((here - back) % count == place, arrived, chosen)
        ordered.append(chosen)
    return jnp.concatenate(ordered, axis=0)


def split_projection(head_values, side_rows):
    own_full, foreign_full = needed_heads(head_values)
    partner = jnp.dot(foreign_full, side_rows, preferred_element_type=jnp.float32)
    outgoing = partner.astype(jnp.bfloat16)
    returned = swapped(outgoing, "dp")
    outgoing, own_full, side_rows = lax.optimization_barrier((outgoing, own_full, side_rows))
    local = jnp.dot(own_full, side_rows, preferred_element_type=jnp.float32)
    local = lax.optimization_barrier(local)
    return local + returned.astype(jnp.float32)


def shards(queries, keyvals, documents, output_weight):
    block_rows = output_weight.shape[0]
    width = queries.shape[2]
    side_width = block_rows * lax.axis_size("ctx")
    fits = lax.axis_size("tensor") == 4
    if lax.axis_size("dp") == 2 and side_width == 2 * width and fits:
        first = ring_step(output_weight, "ctx")
        head_values = attention(queries, keyvals, documents)
        first, head_values = lax.optimization_barrier((first, head_values))
        side_rows = line_rows(output_weight, first, "ctx")
        result = split_projection(head_values, side_rows)
        return result.astype(jnp.bfloat16)[None]
    all_rows = lax.all_gather(output_weight, ("dp", "ctx"), axis=0, tiled=True)
    head_values = attention(queries, keyvals, documents)
    group = lax.axis_size("tensor")
    me = lax.axis_index("tensor")
    result = None
    for distance in range(group):
        held = head_values if distance == 0 else rotated(head_values, "tensor", distance)
        owner = (me - distance) % group
        rows = lax.dynamic_slice_in_dim(all_rows, owner * width, width, 0)
        part = jnp.dot(held, rows, preferred_element_type=jnp.float32)
        result = part if result is None else result + part
    return result.astype(jnp.bfloat16)[None]


def solution(mesh):
    placed = (
        P("dp", "ctx", "tensor"),
        P("dp", "ctx", None, "tensor"),
        P("dp", "ctx"),
        P(("dp", "ctx"), "tensor"),
    )
    return jax.shard_map(
        shards, mesh=mesh, in_specs=placed, out_specs=P("dp", "ctx", "tensor"), check_vma=False
    )
```

```python
import math

import jax
import jax.numpy as jnp
from jax import lax
from jax.sharding import PartitionSpec as P

HEAD_DIM = 128


FLOOR_SCORE = -1e30


def shifted(block, axis, distance):
    devices = range(lax.axis_size(axis))
    route = [(i - distance, i) for i in devices if i - distance in devices]
    return lax.ppermute(block, axis, route)


def rotated(block, axis, distance):
    count = lax.axis_size(axis)
    route = [(i, (i + distance) % count) for i in range(count)]
    return lax.ppermute(block, axis, route)


def attention(queries, keyvals, documents):
    length = queries.shape[1]
    pair_width = keyvals.shape[3]
    pair_heads = pair_width // HEAD_DIM
    query_group_size = queries.shape[2] // pair_width
    cycle_size = lax.axis_size("ctx")
    position = lax.axis_index("ctx")
    offsets = jnp.arange(length, dtype=jnp.int32)
    reach_hops = min(cycle_size - 1, (cycle_size * length // 2 - 1 + length - 1) // length)

    pair_blocks = [keyvals[0]]
    label_blocks = [documents[0]]
    place_blocks = [position * length + offsets]
    if length % pair_width == 0:
        label_rows = documents[0].astype(jnp.bfloat16).reshape(length // pair_width, pair_width)
        packed = jnp.concatenate([keyvals[0].reshape(2 * length, pair_width), label_rows], axis=0)
    else:
        label_slab = jnp.broadcast_to(
            documents[0].astype(jnp.bfloat16)[:, None, None], (length, 1, pair_width)
        )
        packed = jnp.concatenate([keyvals[0], label_slab], axis=1)
    for hop in range(1, reach_hops + 1):
        arrived = shifted(packed, "ctx", hop)
        if length % pair_width == 0:
            pair_blocks.append(arrived[: 2 * length].reshape(length, 2, pair_width))
            label_blocks.append(arrived[2 * length:].reshape(length).astype(jnp.int32))
        else:
            pair_blocks.append(arrived[:, :2])
            label_blocks.append(arrived[:, 2, 0].astype(jnp.int32))
        place_blocks.append((position - hop) * length + offsets)
    pairs = jnp.concatenate(pair_blocks, axis=0)
    key_labels = jnp.concatenate(label_blocks, axis=0)
    key_place = jnp.concatenate(place_blocks, axis=0)
    key_count = pairs.shape[0]

    query_place = position * length + offsets
    query_labels = documents[0]
    query_block = queries[0].reshape(length, pair_heads, query_group_size, HEAD_DIM)
    key_block = pairs[:, 0].reshape(key_count, pair_heads, HEAD_DIM)
    value_block = pairs[:, 1].reshape(key_count, pair_heads, HEAD_DIM)

    scores = jnp.einsum(
        "qhgd,khd->hgqk", query_block, key_block, preferred_element_type=jnp.float32
    )
    scores = scores * (1.0 / math.sqrt(HEAD_DIM))
    allowed = (
        (query_labels[:, None] == key_labels[None, :])
        & (key_place[None, :] <= query_place[:, None])
        & (key_place[None, :] >= 0)
    )
    scores = jnp.where(allowed, scores, FLOOR_SCORE)
    peak = jnp.max(scores, axis=-1, keepdims=True)
    expo = jnp.where(allowed, jnp.exp(scores - peak), 0.0)
    total = jnp.sum(expo, axis=-1)
    summed = jnp.einsum(
        "hgqk,khd->qhgd",
        expo.astype(jnp.bfloat16),
        value_block,
        preferred_element_type=jnp.float32,
    )
    head_values = summed / jnp.transpose(total, (2, 0, 1))[..., None]
    return head_values.reshape(length, pair_heads * query_group_size * HEAD_DIM).astype(
        jnp.bfloat16
    )


def swapped(block, axis):
    return lax.ppermute(block, axis, [(0, 1), (1, 0)])


def sent(block, route):
    return lax.ppermute(block, ("dp", "tensor"), route)


def needed_heads(head_values):
    group = lax.axis_size("tensor")
    me = lax.axis_index("tensor")
    side = lax.axis_index("dp")
    foreign = swapped(head_values, "dp")
    mine = jnp.concatenate([head_values, foreign], axis=1)
    owners = [(s, 2 * s + k) for s in range(2) for k in range(2)]
    over_y = sent(mine, [(s * group + p, s * group + (p ^ 2)) for s, p in owners])
    on_owner = me // 2 == side
    same_core = jnp.where(on_owner, mine, over_y)
    other_core = lax.ppermute(same_core, "tensor", [(t, t ^ 1) for t in range(group)])
    first_core = me % 2 == 0
    width = head_values.shape[1]
    lower = jnp.where(first_core, same_core, other_core)
    upper = jnp.where(first_core, other_core, same_core)
    own_full = jnp.concatenate([lower[:, :width], upper[:, :width]], axis=1)
    foreign_full = jnp.concatenate([lower[:, width:], upper[:, width:]], axis=1)
    return own_full, foreign_full


def ring_step(block, axis):
    count = lax.axis_size(axis)
    return lax.ppermute(block, axis, [(i, (i + 1) % count) for i in range(count)])


def line_rows(block, first, axis):
    count = lax.axis_size(axis)
    here = lax.axis_index(axis)
    arrivals = [(block, 0), (first, 1)]
    carried = first
    for step in range(2, count):
        carried = ring_step(carried, axis)
        arrivals.append((carried, step))
    ordered = []
    for place in range(count):
        chosen = jnp.zeros_like(block)
        for arrived, back in arrivals:
            chosen = jnp.where((here - back) % count == place, arrived, chosen)
        ordered.append(chosen)
    return jnp.concatenate(ordered, axis=0)


def split_projection(head_values, side_rows):
    own_full, foreign_full = needed_heads(head_values)
    partner = jnp.dot(foreign_full, side_rows, preferred_element_type=jnp.float32)
    outgoing = partner.astype(jnp.bfloat16)
    returned = swapped(outgoing, "dp")
    outgoing, own_full, side_rows = lax.optimization_barrier((outgoing, own_full, side_rows))
    local = jnp.dot(own_full, side_rows, preferred_element_type=jnp.float32)
    local = lax.optimization_barrier(local)
    return local + returned.astype(jnp.float32)


def shards(queries, keyvals, documents, output_weight):
    block_rows = output_weight.shape[0]
    width = queries.shape[2]
    side_width = block_rows * lax.axis_size("ctx")
    fits = lax.axis_size("tensor") == 4
    if lax.axis_size("dp") == 2 and side_width == 2 * width and fits:
        first = ring_step(output_weight, "ctx")
        head_values = attention(queries, keyvals, documents)
        first, head_values = lax.optimization_barrier((first, head_values))
        side_rows = line_rows(output_weight, first, "ctx")
        result = split_projection(head_values, side_rows)
        return result.astype(jnp.bfloat16)[None]
    all_rows = lax.all_gather(output_weight, ("dp", "ctx"), axis=0, tiled=True)
    head_values = attention(queries, keyvals, documents)
    group = lax.axis_size("tensor")
    me = lax.axis_index("tensor")
    result = None
    for distance in range(group):
        held = head_values if distance == 0 else rotated(head_values, "tensor", distance)
        owner = (me - distance) % group
        rows = lax.dynamic_slice_in_dim(all_rows, owner * width, width, 0)
        part = jnp.dot(held, rows, preferred_element_type=jnp.float32)
        result = part if result is None else result + part
    return result.astype(jnp.bfloat16)[None]


def solution(mesh):
    placed = (
        P("dp", "ctx", "tensor"),
        P("dp", "ctx", None, "tensor"),
        P("dp", "ctx"),
        P(("dp", "ctx"), "tensor"),
    )
    return jax.shard_map(
        shards, mesh=mesh, in_specs=placed, out_specs=P("dp", "ctx", "tensor"), check_vma=False
    )
```
